256 devices in a mesh: vocab: 32 (over x, z), fsdp: 8 (over y, core).
Axes of the slice: x: 4, y: 4, z: 8, core: 2. Of those that a mesh axis runs over, the one named last changes fastest.
Arguments:
- hidden: bfloat16 [131072, 2048], P(('vocab', 'fsdp')), may hold values from -100 to 100
- head_weight: bfloat16 [262144, 2048], P(('vocab', 'fsdp')), may hold values from -2.5 to 2.5
- language_blocks: int32 [256, 6], replicated, may hold values from 0 to 7, as said below
- language_owner: int32 [256], replicated, may hold values from 0 to 255, each once
- token_language: int32 [131072, 1], P(('vocab', 'fsdp')), may hold values from 0 to 255; in each aligned block of 512 rows (0 to 511, 512 to 1023, ...) at most 4 rows name the same one
- labels: int32 [131072], P(('vocab', 'fsdp')), may hold values from 0 to 767
- loss_weight: bfloat16 [131072], P(('vocab', 'fsdp')), may hold values from 1 to 16
Outputs:
- hidden_grad: bfloat16 [131072, 2048], P(('vocab', 'fsdp'))
- token_loss: bfloat16 [131072], P(('vocab', 'fsdp'))
- head_grad: bfloat16 [262144, 2048], P(('vocab', 'fsdp'))
The draws below stay inside these ranges and needn't reach their ends.
Inputs may be any that keep to these rules, and one draw needn't show every extreme that they name: `language_blocks`: each row names 6 different blocks. `language_owner`: each language slot is named by exactly one language. `token_language`: in each aligned group of 512 tokens no language is named more than 4 times, a bound that some block reaches in some or all groups.
All inputs are finite; a program needn't handle non-finite values.
Results may differ from the reference program's by a relative error of at most 0.0049.
Values may be sent and summed in bfloat16 or wider, within the bound.
No kernel may reach another device: no remote copies, remote signals or barrier semaphores. Data moves between devices by JAX's collectives and lax.ppermute only.
A program may use at most 128 MiB of HBM per device.

```python
import math
import jax
import jax.numpy as jnp
import numpy as np
from jax import lax

D = 2048
BLOCK = 128
LANGS = 256
SB = 8
LB = 6
TOK_DEV = 512
CAP = 4
TOKENS = 131072
VOCAB = 262144
N_VOCAB = 32
N_FSDP = 8


def draw_hidden(key, part):
    noise_key = jax.random.fold_in(key, 11)
    values = jax.random.truncated_normal(noise_key, -5.0, 5.0, (TOKENS, D), jnp.float32)
    return values.astype(jnp.bfloat16)


def draw_head_weight(key, part):
    noise_key = jax.random.fold_in(key, 21)
    values = jax.random.truncated_normal(noise_key, -5.0, 5.0, (VOCAB, D), jnp.float32) * (3.0 / math.sqrt(D))
    return values.astype(jnp.bfloat16)


def draw_language_blocks(key, part):
    row_keys = jax.random.split(jax.random.fold_in(key, 31), LANGS)
    chosen = jax.vmap(lambda subkey: jax.random.permutation(subkey, SB)[:LB])(row_keys)
    return chosen.astype(jnp.int32)


def with_ends(entries, own_key, least, largest):
    place = [jax.random.randint(jax.random.fold_in(own_key, axis), (), 0, length) for axis, length in enumerate(entries.shape)]
    widest = entries.shape.index(max(entries.shape))
    neighbour = place[:widest] + [(place[widest] + 1) % entries.shape[widest]] + place[widest + 1:]
    return entries.at[tuple(place)].set(least).at[tuple(neighbour)].set(largest)


def steps_of(rng, dims, shards, low, top_value):
    gain, own = 1.0, jax.random.fold_in(rng, 6)
    for dim, shards_of in shards:
        steps = jnp.exp(jax.random.uniform(jax.random.fold_in(own, dim), (shards_of,), jnp.float32, low / len(shards), top_value / len(shards)))
        gain = gain * jnp.repeat(steps, dims[dim] // shards_of).reshape([-1 if axis == dim else 1 for axis in range(len(dims))])
    return gain


def shared_out(rng, own, number, rows, count, top, most, lean):
    order = jax.random.permutation(rng, count)
    packed, common = shares(count, rows * top, most, lean, True), shares(count, rows * top, most, lean, False)
    places = jnp.arange(count)

    def named(sizes, turn):
        used = int((sizes > 0).sum())
        fixed = max(1, used // 4)
        passed = fixed + (places - fixed + turn * (used - fixed)) % max(1, count - fixed)
        return jnp.zeros((count,), jnp.int32).at[order[jnp.where(places < fixed, places, passed)]].set(jnp.asarray(sizes, jnp.int32))

    sizes = jnp.where(number % 4 == 0, named(packed, number // 4), named(common, number - number // 4 - 1))
    mixed = jax.random.permutation(jax.random.fold_in(own, 3), count)
    source_of, sink = mixed[0:count // 2 * 2:2], mixed[1:count // 2 * 2:2]
    room = jnp.minimum(sizes[source_of] - 1, most - sizes[sink]) // 2
    room = jnp.where((source_of == order[0]) | (sink == order[0]) | (sizes[sink] == 0), 0, jnp.maximum(room, 0))
    passed = jax.random.randint(jax.random.fold_in(own, 4), (count // 2,), 0, 1 << 20) % (room + 1)
    sizes = sizes.at[source_of].add(-passed).at[sink].add(passed)
    members = jnp.searchsorted(jnp.cumsum(sizes), jnp.arange(rows * top), side="right").astype(jnp.int32)
    grid = members.reshape(top, rows).T
    grid = grid[jax.random.permutation(jax.random.fold_in(own, 1), rows)]
    turn = jax.random.randint(jax.random.fold_in(own, 2), (rows, 1), 0, top)
    return jnp.take_along_axis(grid, (jnp.arange(top)[None, :] + turn) % top, axis=1)


def shares(amount, total, limit, skew, full):
    weights = [(1 << 20) // math.isqrt(grade ** skew) + 1 for grade in range(1, amount + 1)]
    largest = limit if full else min(limit, max(-(-total // amount), total * weights[0] // sum(weights)))
    least = 1 if total - largest >= amount - 1 else 0
    given, spare = [largest] + [least] * (amount - 1), total - largest - least * (amount - 1)
    while spare > 0:
        movable = [i for i in range(1, amount) if given[i] < largest] or [i for i in range(1, amount) if given[i] < limit]
        pool, remaining = sum([weights[i] for i in movable]), spare
        for i in movable:
            more = min(limit - given[i], max(1, remaining * weights[i] // pool), spare)
            given[i] = given[i] + more
            spare = spare - more
    return np.array(given)


def setup_inputs(seed: int = 0) -> dict:
    seeds = jax.random.split(jax.random.key(seed), 8)
    hidden = draw_hidden(jax.random.fold_in(seeds[7], 71), 0)
    head_weight = draw_head_weight(jax.random.fold_in(seeds[7], 71), 0)
    language_blocks = draw_language_blocks(jax.random.fold_in(seeds[7], 71), 0)
    language_owner = jax.random.permutation(seeds[3], LANGS).astype(jnp.int32)
    token_language_keys = jax.random.split(jax.random.fold_in(seeds[4], 1), TOKENS // TOK_DEV)
    token_language_turns = jax.random.permutation(jax.random.fold_in(seeds[4], 3), TOKENS // TOK_DEV)
    token_language = jax.vmap(lambda own, number: shared_out(jax.random.fold_in(seeds[4], 2), own, number, TOK_DEV, LANGS, 1, CAP, 2))(token_language_keys, token_language_turns).reshape((TOKENS, 1))
    labels = with_ends(jax.random.randint(seeds[5], (TOKENS,), 0, LB * BLOCK), jax.random.fold_in(seeds[5], 1), 0, (LB * BLOCK) - 1).astype(jnp.int32)
    loss_weight = jnp.clip(jnp.exp(math.log(16.0) - 2.7725887 * jax.random.uniform(seeds[6], (TOKENS,), jnp.float32) ** steps_of(seeds[6], (TOKENS,), ((0, 256),), -0.2, 0.2)), 1.0, 16.0).astype(jnp.bfloat16)
    return dict(hidden=hidden, head_weight=head_weight, language_blocks=language_blocks, language_owner=language_owner, token_language=token_language, labels=labels, loss_weight=loss_weight)


SMOOTH = 0.1


def smoothed_loss(logits, targets, weights):
    columns = logits.shape[1]
    row_max = jnp.max(logits, axis=1, keepdims=True)
    shifted = logits - row_max
    log_probs = shifted - jnp.log(jnp.sum(jnp.exp(shifted), axis=1, keepdims=True))
    onehot = (lax.broadcasted_iota(jnp.int32, logits.shape, 1) == targets[:, None]).astype(jnp.float32)
    losses = -(1.0 - SMOOTH) * jnp.sum(onehot * log_probs, axis=1) - (SMOOTH / columns) * jnp.sum(log_probs, axis=1)
    grads = weights.astype(jnp.float32)[:, None] * (jnp.exp(log_probs) - (1.0 - SMOOTH) * onehot - SMOOTH / columns)
    return losses.astype(jnp.bfloat16), grads.astype(jnp.bfloat16)


def slot_work(token_rows, weights, targets, slot_weights, blocks):
    candidates = jnp.take(slot_weights, blocks, axis=0).reshape(LB * BLOCK, D)
    logits = lax.dot_general(token_rows, candidates, (((1,), (1,)), ((), ())), preferred_element_type=jnp.float32)
    losses, grads = smoothed_loss(logits, targets, weights)
    row_grads = jnp.dot(grads, candidates, preferred_element_type=jnp.float32).astype(jnp.bfloat16)
    cand_grads = lax.dot_general(grads, token_rows, (((0,), (0,)), ((), ())), preferred_element_type=jnp.float32)
    slab_grads = jnp.zeros((SB, BLOCK, D), jnp.float32).at[blocks].add(cand_grads.reshape(LB, BLOCK, D))
    return row_grads, losses, slab_grads.astype(jnp.bfloat16)


def reference(hidden, head_weight, language_blocks, language_owner, token_language, labels, loss_weight):
    devices = N_VOCAB * N_FSDP
    language = token_language[:, 0]
    slot_ids = jnp.take(language_owner, language, axis=0)
    grouped = language.reshape(devices, TOK_DEV)
    positions = jnp.arange(TOK_DEV, dtype=jnp.int32)
    earlier = (grouped[:, :, None] == grouped[:, None, :]) & (positions[None, None, :] < positions[None, :, None])
    rank_in_group = jnp.sum(earlier.astype(jnp.int32), axis=2).reshape(TOKENS)
    source = jnp.arange(TOKENS, dtype=jnp.int32) // TOK_DEV
    position = source * CAP + rank_in_group
    places = devices * CAP
    language_of = jnp.zeros((LANGS,), jnp.int32).at[language_owner].set(jnp.arange(LANGS, dtype=jnp.int32))
    slab_weights = head_weight.reshape(LANGS, SB, BLOCK, D)
    token_ids = jnp.arange(TOKENS, dtype=jnp.int32)

    def slot_step(running, slot_items):
        hidden_grad, token_loss = running
        slot_index, slot_weights = slot_items
        target_place = jnp.where(slot_ids == slot_index, position, places)
        row_index = jnp.full((places,), TOKENS, jnp.int32).at[target_place].set(token_ids, mode="drop")
        token_rows = jnp.take(hidden, row_index, axis=0, mode="fill", fill_value=0)
        weights = jnp.take(loss_weight, row_index, axis=0, mode="fill", fill_value=0)
        targets = jnp.take(labels, row_index, axis=0, mode="fill", fill_value=0)
        blocks = jnp.take(language_blocks, language_of[slot_index], axis=0)
        row_grads, losses, slab_grads = slot_work(token_rows, weights, targets, slot_weights, blocks)
        hidden_grad = hidden_grad.at[row_index].set(row_grads, mode="drop")
        token_loss = token_loss.at[row_index].set(losses, mode="drop")
        return (hidden_grad, token_loss), slab_grads

    start_state = (jnp.zeros((TOKENS, D), jnp.bfloat16), jnp.zeros((TOKENS,), jnp.bfloat16))
    (hidden_grad, token_loss), head_grads = lax.scan(slot_step, start_state, (jnp.arange(LANGS, dtype=jnp.int32), slab_weights))
    return hidden_grad, token_loss, head_grads.reshape(VOCAB, D)
```

```python
import jax
import jax.numpy as jnp
from jax import lax
from jax.sharding import PartitionSpec as P

D = 2048
BLOCK = 128
SB = 8
LB = 6
CAP = 4
EXTRA = 128
LABEL_SPLIT = 128

SMOOTH = 0.1
AXES = ("vocab", "fsdp")


def smoothed_loss(logits, targets, weights):
    columns = logits.shape[1]
    row_max = jnp.max(logits, axis=1, keepdims=True)
    shifted = logits - row_max
    log_probs = shifted - jnp.log(jnp.sum(jnp.exp(shifted), axis=1, keepdims=True))
    onehot = (lax.broadcasted_iota(jnp.int32, logits.shape, 1) == targets[:, None]).astype(
        jnp.float32
    )
    losses = -(1.0 - SMOOTH) * jnp.sum(onehot * log_probs, axis=1) - SMOOTH / columns * jnp.sum(
        log_probs, axis=1
    )
    grads = weights.astype(jnp.float32)[:, None] * (
        jnp.exp(log_probs) - (1.0 - SMOOTH) * onehot - SMOOTH / columns
    )
    return (losses.astype(jnp.bfloat16), grads.astype(jnp.bfloat16))


def place_tokens(token_language, language_owner):
    language = token_language[:, 0]
    languages = language_owner.shape[0]
    matches = language[:, None] == jnp.arange(languages, dtype=jnp.int32)[None, :]
    slot_ids = jnp.sum(jnp.where(matches, language_owner[None, :], 0), axis=1)
    positions = jnp.arange(language.shape[0], dtype=jnp.int32)
    earlier = (language[:, None] == language[None, :]) & (positions[None, :] < positions[:, None])
    rank_in_group = jnp.sum(earlier.astype(jnp.int32), axis=1)
    return slot_ids * CAP + rank_in_group


def shards(
    hidden, head_weight, language_blocks, language_owner, token_language, labels, loss_weight
):
    devices = lax.axis_size(AXES)
    tokens, features = hidden.shape
    places = devices * CAP
    width = features + EXTRA
    assert head_weight.shape[0] == SB * BLOCK

    target_place = place_tokens(token_language, language_owner)
    place_hot = (
        lax.broadcasted_iota(jnp.int32, (places, tokens), 0) == target_place[None, :]
    ).astype(jnp.bfloat16)

    extra_cols = lax.broadcasted_iota(jnp.int32, (tokens, EXTRA), 1)
    label_hi = (labels // LABEL_SPLIT).astype(jnp.bfloat16)
    label_lo = (labels % LABEL_SPLIT).astype(jnp.bfloat16)
    extras = jnp.where(
        extra_cols == 0,
        loss_weight[:, None],
        jnp.where(
            extra_cols == 1,
            label_hi[:, None],
            jnp.where(extra_cols == 2, label_lo[:, None], jnp.zeros((), jnp.bfloat16)),
        ),
    )
    packed = jnp.concatenate([hidden, extras], axis=1)
    send = jnp.dot(place_hot, packed, preferred_element_type=jnp.float32).astype(jnp.bfloat16)

    received = lax.all_to_all(
        send.reshape(devices, CAP, width), AXES, split_axis=0, concat_axis=0, tiled=True
    ).reshape(places, width)

    token_rows = received[:, :features]
    weights = received[:, features]
    targets = (
        received[:, features + 1].astype(jnp.int32) * LABEL_SPLIT
        + received[:, features + 2].astype(jnp.int32)
    )

    self_index = lax.axis_index(AXES)
    owned_mask = (language_owner == self_index).astype(jnp.int32)
    blocks = jnp.sum(owned_mask[:, None] * language_blocks, axis=0)
    slab = head_weight.reshape(SB, BLOCK, features)
    candidates = jnp.take(slab, blocks, axis=0).reshape(LB * BLOCK, features)

    logits = lax.dot_general(
        token_rows, candidates, (((1,), (1,)), ((), ())), preferred_element_type=jnp.float32
    )
    losses, grads = smoothed_loss(logits, targets, weights)
    row_grads = jnp.dot(grads, candidates, preferred_element_type=jnp.float32).astype(
        jnp.bfloat16
    )

    block_hot = blocks[None, :] == jnp.arange(SB, dtype=jnp.int32)[:, None]
    listed = jnp.any(block_hot, axis=1)
    list_index = jnp.sum(
        jnp.where(block_hot, jnp.arange(LB, dtype=jnp.int32)[None, :], 0), axis=1
    )
    grads_by_block = grads.reshape(places, LB, BLOCK)
    expanded = jnp.where(
        listed[None, :, None],
        jnp.take(grads_by_block, list_index, axis=1),
        jnp.zeros((), jnp.bfloat16),
    ).reshape(places, SB * BLOCK)
    head_grad = lax.dot_general(
        expanded, token_rows, (((0,), (0,)), ((), ())), preferred_element_type=jnp.float32
    ).astype(jnp.bfloat16)

    back_cols = lax.broadcasted_iota(jnp.int32, (places, EXTRA), 1)
    back_extras = jnp.where(back_cols == 0, losses[:, None], jnp.zeros((), jnp.bfloat16))
    back = jnp.concatenate([row_grads, back_extras], axis=1)
    returned = lax.all_to_all(
        back.reshape(devices, CAP, width), AXES, split_axis=0, concat_axis=0, tiled=True
    ).reshape(places, width)

    gathered = lax.dot_general(
        place_hot, returned, (((0,), (0,)), ((), ())), preferred_element_type=jnp.float32
    )
    hidden_grad = gathered[:, :features].astype(jnp.bfloat16)
    token_loss = gathered[:, features].astype(jnp.bfloat16)
    return (hidden_grad, token_loss, head_grad)


def solution(mesh):
    in_specs = (
        P(AXES, None),
        P(AXES, None),
        P(),
        P(),
        P(AXES, None),
        P(AXES),
        P(AXES),
    )
    out_specs = (P(AXES, None), P(AXES), P(AXES, None))
    return jax.shard_map(shards, mesh=mesh, in_specs=in_specs, out_specs=out_specs, check_vma=False)
```

```python
import jax
import jax.numpy as jnp
from jax import lax
from jax.sharding import PartitionSpec as P

D = 2048
BLOCK = 128
SB = 8
LB = 6
CAP = 4
EXTRA = 128
LABEL_SPLIT = 128
SPLIT = 1024

SMOOTH = 0.1
AXES = ("vocab", "fsdp")


def smoothed_loss(logits, targets, weights):
    columns = logits.shape[1]
    row_max = jnp.max(logits, axis=1, keepdims=True)
    shifted = logits - row_max
    log_probs = shifted - jnp.log(jnp.sum(jnp.exp(shifted), axis=1, keepdims=True))
    onehot = (lax.broadcasted_iota(jnp.int32, logits.shape, 1) == targets[:, None]).astype(
        jnp.float32
    )
    losses = -(1.0 - SMOOTH) * jnp.sum(onehot * log_probs, axis=1) - SMOOTH / columns * jnp.sum(
        log_probs, axis=1
    )
    grads = weights.astype(jnp.float32)[:, None] * (
        jnp.exp(log_probs) - (1.0 - SMOOTH) * onehot - SMOOTH / columns
    )
    return (losses.astype(jnp.bfloat16), grads.astype(jnp.bfloat16))


def place_tokens(token_language, language_owner):
    language = token_language[:, 0]
    languages = language_owner.shape[0]
    matches = language[:, None] == jnp.arange(languages, dtype=jnp.int32)[None, :]
    slot_ids = jnp.sum(jnp.where(matches, language_owner[None, :], 0), axis=1)
    positions = jnp.arange(language.shape[0], dtype=jnp.int32)
    earlier = (language[:, None] == language[None, :]) & (positions[None, :] < positions[:, None])
    rank_in_group = jnp.sum(earlier.astype(jnp.int32), axis=1)
    return slot_ids * CAP + rank_in_group


def shards(
    hidden, head_weight, language_blocks, language_owner, token_language, labels, loss_weight
):
    devices = lax.axis_size(AXES)
    tokens, features = hidden.shape
    places = devices * CAP
    width = features + EXTRA
    assert head_weight.shape[0] == SB * BLOCK

    target_place = place_tokens(token_language, language_owner)
    place_hot = (
        lax.broadcasted_iota(jnp.int32, (places, tokens), 0) == target_place[None, :]
    ).astype(jnp.bfloat16)

    extra_cols = lax.broadcasted_iota(jnp.int32, (tokens, EXTRA), 1)
    label_hi = (labels // LABEL_SPLIT).astype(jnp.bfloat16)
    label_lo = (labels % LABEL_SPLIT).astype(jnp.bfloat16)
    extras = jnp.where(
        extra_cols == 0,
        loss_weight[:, None],
        jnp.where(
            extra_cols == 1,
            label_hi[:, None],
            jnp.where(extra_cols == 2, label_lo[:, None], jnp.zeros((), jnp.bfloat16)),
        ),
    )
    packed = jnp.concatenate([hidden, extras], axis=1)
    bounds = [(0, SPLIT), (SPLIT, width)]

    def exchange(values):
        return lax.all_to_all(
            values.reshape(devices, CAP, values.shape[1]), AXES, split_axis=0, concat_axis=0,
            tiled=True,
        ).reshape(places, values.shape[1])

    received = []
    for lo, hi in bounds:
        send = jnp.dot(place_hot, packed[:, lo:hi], preferred_element_type=jnp.float32)
        received.append(exchange(send.astype(jnp.bfloat16)))
    tail = received[-1]
    weights = tail[:, features - SPLIT]
    targets = (
        tail[:, features - SPLIT + 1].astype(jnp.int32) * LABEL_SPLIT
        + tail[:, features - SPLIT + 2].astype(jnp.int32)
    )

    self_index = lax.axis_index(AXES)
    owned_mask = (language_owner == self_index).astype(jnp.int32)
    blocks = jnp.sum(owned_mask[:, None] * language_blocks, axis=0)
    slab = head_weight.reshape(SB, BLOCK, features)
    candidates = jnp.take(slab, blocks, axis=0).reshape(LB * BLOCK, features)
    cand_padded = jnp.concatenate(
        [candidates, jnp.zeros((LB * BLOCK, EXTRA), jnp.bfloat16)], axis=1
    )

    logits = None
    for (lo, hi), part in zip(bounds, received):
        piece = lax.dot_general(
            part, cand_padded[:, lo:hi], (((1,), (1,)), ((), ())),
            preferred_element_type=jnp.float32,
        )
        logits = piece if logits is None else logits + piece
    losses, grads = smoothed_loss(logits, targets, weights)

    back_cols = lax.broadcasted_iota(jnp.int32, (places, EXTRA), 1)
    returned = []
    for lo, hi in bounds:
        part = jnp.dot(grads, cand_padded[:, lo:hi], preferred_element_type=jnp.float32)
        part = part.astype(jnp.bfloat16)
        if hi == width:
            part = jnp.where(
                (lax.broadcasted_iota(jnp.int32, part.shape, 1) == features - lo),
                losses[:, None],
                part,
            )
        returned.append(exchange(part))

    block_hot = blocks[None, :] == jnp.arange(SB, dtype=jnp.int32)[:, None]
    listed = jnp.any(block_hot, axis=1)
    list_index = jnp.sum(
        jnp.where(block_hot, jnp.arange(LB, dtype=jnp.int32)[None, :], 0), axis=1
    )
    grads_by_block = grads.reshape(places, LB, BLOCK)
    expanded = jnp.where(
        listed[None, :, None],
        jnp.take(grads_by_block, list_index, axis=1),
        jnp.zeros((), jnp.bfloat16),
    ).reshape(places, SB * BLOCK)
    token_rows = jnp.concatenate([received[0], received[1][:, : features - SPLIT]], axis=1)
    head_grad = lax.dot_general(
        expanded, token_rows, (((0,), (0,)), ((), ())), preferred_element_type=jnp.float32
    ).astype(jnp.bfloat16)

    gathered = [
        lax.dot_general(
            place_hot, part, (((0,), (0,)), ((), ())), preferred_element_type=jnp.float32
        )
        for part in returned
    ]
    hidden_grad = jnp.concatenate(
        [gathered[0], gathered[1][:, : features - SPLIT]], axis=1
    ).astype(jnp.bfloat16)
    token_loss = gathered[1][:, features - SPLIT].astype(jnp.bfloat16)
    return (hidden_grad, token_loss, head_grad)


def solution(mesh):
    in_specs = (
        P(AXES, None),
        P(AXES, None),
        P(),
        P(),
        P(AXES, None),
        P(AXES),
        P(AXES),
    )
    out_specs = (P(AXES, None), P(AXES), P(AXES, None))
    return jax.shard_map(shards, mesh=mesh, in_specs=in_specs, out_specs=out_specs, check_vma=False)
```

```python
import jax
import jax.numpy as jnp
from jax import lax
from jax.experimental import pallas as pl
from jax.sharding import PartitionSpec as P

D = 2048
BLOCK = 128
SB = 8
LB = 6
CAP = 4
EXTRA = 128
LABEL_SPLIT = 128

SMOOTH = 0.1
AXES = ("vocab", "fsdp")
GROUPS_PER_STEP = 64


def _split_rows(x_ref, o_ref):
    x = x_ref[...]
    o_ref[...] = x.reshape(o_ref.shape)


def _join_rows(x_ref, o_ref):
    x = x_ref[...]
    o_ref[...] = x.reshape(o_ref.shape)


def to_groups(x):
    rows, width = x.shape
    groups = rows // CAP
    step = min(GROUPS_PER_STEP, groups)
    return pl.pallas_call(
        _split_rows,
        grid=(groups // step,),
        in_specs=[pl.BlockSpec((step * CAP, width), lambda i: (i, 0))],
        out_specs=pl.BlockSpec((step, CAP, width), lambda i: (i, 0, 0)),
        out_shape=jax.ShapeDtypeStruct((groups, CAP, width), x.dtype),
    )(x)


def from_groups(x):
    groups, cap, width = x.shape
    step = min(GROUPS_PER_STEP, groups)
    return pl.pallas_call(
        _join_rows,
        grid=(groups // step,),
        in_specs=[pl.BlockSpec((step, cap, width), lambda i: (i, 0, 0))],
        out_specs=pl.BlockSpec((step * cap, width), lambda i: (i, 0)),
        out_shape=jax.ShapeDtypeStruct((groups * cap, width), x.dtype),
    )(x)


def smoothed_loss(logits, targets, weights):
    columns = logits.shape[1]
    row_max = jnp.max(logits, axis=1, keepdims=True)
    shifted = logits - row_max
    log_probs = shifted - jnp.log(jnp.sum(jnp.exp(shifted), axis=1, keepdims=True))
    onehot = (lax.broadcasted_iota(jnp.int32, logits.shape, 1) == targets[:, None]).astype(
        jnp.float32
    )
    losses = -(1.0 - SMOOTH) * jnp.sum(onehot * log_probs, axis=1) - SMOOTH / columns * jnp.sum(
        log_probs, axis=1
    )
    grads = weights.astype(jnp.float32)[:, None] * (
        jnp.exp(log_probs) - (1.0 - SMOOTH) * onehot - SMOOTH / columns
    )
    return (losses.astype(jnp.bfloat16), grads.astype(jnp.bfloat16))


def place_tokens(token_language, language_owner):
    language = token_language[:, 0]
    languages = language_owner.shape[0]
    matches = language[:, None] == jnp.arange(languages, dtype=jnp.int32)[None, :]
    slot_ids = jnp.sum(jnp.where(matches, language_owner[None, :], 0), axis=1)
    positions = jnp.arange(language.shape[0], dtype=jnp.int32)
    earlier = (language[:, None] == language[None, :]) & (positions[None, :] < positions[:, None])
    rank_in_group = jnp.sum(earlier.astype(jnp.int32), axis=1)
    return slot_ids * CAP + rank_in_group


def shards(
    hidden, head_weight, language_blocks, language_owner, token_language, labels, loss_weight
):
    devices = lax.axis_size(AXES)
    tokens, features = hidden.shape
    places = devices * CAP
    width = features + EXTRA
    assert head_weight.shape[0] == SB * BLOCK

    target_place = place_tokens(token_language, language_owner)
    place_hot = (
        lax.broadcasted_iota(jnp.int32, (places, tokens), 0) == target_place[None, :]
    ).astype(jnp.bfloat16)

    extra_cols = lax.broadcasted_iota(jnp.int32, (tokens, EXTRA), 1)
    label_hi = (labels // LABEL_SPLIT).astype(jnp.bfloat16)
    label_lo = (labels % LABEL_SPLIT).astype(jnp.bfloat16)
    extras = jnp.where(
        extra_cols == 0,
        loss_weight[:, None],
        jnp.where(
            extra_cols == 1,
            label_hi[:, None],
            jnp.where(extra_cols == 2, label_lo[:, None], jnp.zeros((), jnp.bfloat16)),
        ),
    )
    packed = jnp.concatenate([hidden, extras], axis=1)
    send = jnp.dot(place_hot, packed, preferred_element_type=jnp.float32).astype(jnp.bfloat16)

    received = from_groups(
        lax.all_to_all(to_groups(send), AXES, split_axis=0, concat_axis=0, tiled=True)
    )

    token_rows = received[:, :features]
    weights = received[:, features]
    targets = (
        received[:, features + 1].astype(jnp.int32) * LABEL_SPLIT
        + received[:, features + 2].astype(jnp.int32)
    )

    self_index = lax.axis_index(AXES)
    owned_mask = (language_owner == self_index).astype(jnp.int32)
    blocks = jnp.sum(owned_mask[:, None] * language_blocks, axis=0)
    slab = head_weight.reshape(SB, BLOCK, features)
    candidates = jnp.take(slab, blocks, axis=0).reshape(LB * BLOCK, features)

    logits = lax.dot_general(
        token_rows, candidates, (((1,), (1,)), ((), ())), preferred_element_type=jnp.float32
    )
    losses, grads = smoothed_loss(logits, targets, weights)
    cand_padded = jnp.concatenate(
        [candidates, jnp.zeros((LB * BLOCK, EXTRA), jnp.bfloat16)], axis=1
    )
    row_grads = jnp.dot(grads, cand_padded, preferred_element_type=jnp.float32).astype(
        jnp.bfloat16
    )
    back = jnp.where(
        lax.broadcasted_iota(jnp.int32, row_grads.shape, 1) == features, losses[:, None], row_grads
    )

    block_hot = blocks[None, :] == jnp.arange(SB, dtype=jnp.int32)[:, None]
    listed = jnp.any(block_hot, axis=1)
    list_index = jnp.sum(
        jnp.where(block_hot, jnp.arange(LB, dtype=jnp.int32)[None, :], 0), axis=1
    )
    grads_by_block = grads.reshape(places, LB, BLOCK)
    expanded = jnp.where(
        listed[None, :, None],
        jnp.take(grads_by_block, list_index, axis=1),
        jnp.zeros((), jnp.bfloat16),
    ).reshape(places, SB * BLOCK)
    head_grad = lax.dot_general(
        expanded, token_rows, (((0,), (0,)), ((), ())), preferred_element_type=jnp.float32
    ).astype(jnp.bfloat16)

    returned = from_groups(
        lax.all_to_all(to_groups(back), AXES, split_axis=0, concat_axis=0, tiled=True)
    )

    hidden_grad = lax.dot_general(
        place_hot, returned[:, :features], (((0,), (0,)), ((), ())),
        preferred_element_type=jnp.float32,
    ).astype(jnp.bfloat16)
    token_loss = lax.dot_general(
        place_hot, returned[:, features:], (((0,), (0,)), ((), ())),
        preferred_element_type=jnp.float32,
    )[:, 0].astype(jnp.bfloat16)
    return (hidden_grad, token_loss, head_grad)


def solution(mesh):
    in_specs = (
        P(AXES, None),
        P(AXES, None),
        P(),
        P(),
        P(AXES, None),
        P(AXES),
        P(AXES),
    )
    out_specs = (P(AXES, None), P(AXES), P(AXES, None))
    return jax.shard_map(shards, mesh=mesh, in_specs=in_specs, out_specs=out_specs, check_vma=False)
```

```python
import jax
import jax.numpy as jnp
from jax import lax
from jax.experimental import pallas as pl
from jax.sharding import PartitionSpec as P

D = 2048
BLOCK = 128
SB = 8
LB = 6
CAP = 4
EXTRA = 128
LABEL_SPLIT = 128

SMOOTH = 0.1
AXES = ("vocab", "fsdp")
GROUPS_PER_STEP = 64


def place_tokens(token_language, language_owner):
    language = token_language[:, 0]
    languages = language_owner.shape[0]
    matches = language[:, None] == jnp.arange(languages, dtype=jnp.int32)[None, :]
    slot_ids = jnp.sum(jnp.where(matches, language_owner[None, :], 0), axis=1)
    positions = jnp.arange(language.shape[0], dtype=jnp.int32)
    earlier = (language[:, None] == language[None, :]) & (positions[None, :] < positions[:, None])
    rank_in_group = jnp.sum(earlier.astype(jnp.int32), axis=1)
    return slot_ids * CAP + rank_in_group


def _split_rows(x_ref, o_ref):
    x = x_ref[...]
    o_ref[...] = x.reshape(o_ref.shape)


def _join_rows(x_ref, o_ref):
    x = x_ref[...]
    o_ref[...] = x.reshape(o_ref.shape)


def to_groups(x):
    rows, width = x.shape
    groups = rows // CAP
    step = min(GROUPS_PER_STEP, groups)
    return pl.pallas_call(
        _split_rows,
        grid=(groups // step,),
        in_specs=[pl.BlockSpec((step * CAP, width), lambda i: (i, 0))],
        out_specs=pl.BlockSpec((step, CAP, width), lambda i: (i, 0, 0)),
        out_shape=jax.ShapeDtypeStruct((groups, CAP, width), x.dtype),
    )(x)


def from_groups(x):
    groups, cap, width = x.shape
    step = min(GROUPS_PER_STEP, groups)
    return pl.pallas_call(
        _join_rows,
        grid=(groups // step,),
        in_specs=[pl.BlockSpec((step, cap, width), lambda i: (i, 0, 0))],
        out_specs=pl.BlockSpec((step * cap, width), lambda i: (i, 0)),
        out_shape=jax.ShapeDtypeStruct((groups * cap, width), x.dtype),
    )(x)


def _middle(r_ref, cand_ref, back_ref, rows_ref, grads_ref):
    x = r_ref[...]
    x = x.reshape(x.shape[0] * x.shape[1], x.shape[2])
    rows_ref[...] = x
    n, width = x.shape
    cand = cand_ref[...]
    columns, features = cand.shape
    logits = lax.dot_general(
        x[:, :features], cand, (((1,), (1,)), ((), ())), preferred_element_type=jnp.float32
    )
    weights = x[:, features : features + 1].astype(jnp.float32)
    targets = (
        x[:, features + 1 : features + 2].astype(jnp.float32) * LABEL_SPLIT
        + x[:, features + 2 : features + 3].astype(jnp.float32)
    ).astype(jnp.int32)
    row_max = jnp.max(logits, axis=1, keepdims=True)
    shifted = logits - row_max
    log_probs = shifted - jnp.log(jnp.sum(jnp.exp(shifted), axis=1, keepdims=True))
    onehot = (lax.broadcasted_iota(jnp.int32, logits.shape, 1) == targets).astype(jnp.float32)
    losses = -(1.0 - SMOOTH) * jnp.sum(onehot * log_probs, axis=1, keepdims=True) - (
        SMOOTH / columns
    ) * jnp.sum(log_probs, axis=1, keepdims=True)
    grads = (
        weights * (jnp.exp(log_probs) - (1.0 - SMOOTH) * onehot - SMOOTH / columns)
    ).astype(jnp.bfloat16)
    grads_ref[...] = grads
    row_grads = jnp.dot(grads, cand, preferred_element_type=jnp.float32).astype(jnp.bfloat16)
    extras = jnp.where(
        lax.broadcasted_iota(jnp.int32, (n, width - features), 1) == 0,
        losses.astype(jnp.bfloat16),
        jnp.zeros((), jnp.bfloat16),
    )
    back = jnp.concatenate([row_grads, extras], axis=1)
    back_ref[...] = back.reshape(back_ref.shape)


def middle(received, candidates):
    groups, cap, width = received.shape
    columns, features = candidates.shape
    step = min(GROUPS_PER_STEP, groups)
    return pl.pallas_call(
        _middle,
        grid=(groups // step,),
        in_specs=[
            pl.BlockSpec((step, cap, width), lambda i: (i, 0, 0)),
            pl.BlockSpec((columns, features), lambda i: (0, 0)),
        ],
        out_specs=[
            pl.BlockSpec((step, cap, width), lambda i: (i, 0, 0)),
            pl.BlockSpec((step * cap, width), lambda i: (i, 0)),
            pl.BlockSpec((step * cap, columns), lambda i: (i, 0)),
        ],
        out_shape=[
            jax.ShapeDtypeStruct((groups, cap, width), received.dtype),
            jax.ShapeDtypeStruct((groups * cap, width), received.dtype),
            jax.ShapeDtypeStruct((groups * cap, columns), jnp.bfloat16),
        ],
    )(received, candidates)


def shards(
    hidden, head_weight, language_blocks, language_owner, token_language, labels, loss_weight
):
    devices = lax.axis_size(AXES)
    tokens, features = hidden.shape
    places = devices * CAP
    assert head_weight.shape[0] == SB * BLOCK

    target_place = place_tokens(token_language, language_owner)
    place_hot = (
        lax.broadcasted_iota(jnp.int32, (places, tokens), 0) == target_place[None, :]
    ).astype(jnp.bfloat16)

    extra_cols = lax.broadcasted_iota(jnp.int32, (tokens, EXTRA), 1)
    label_hi = (labels // LABEL_SPLIT).astype(jnp.bfloat16)
    label_lo = (labels % LABEL_SPLIT).astype(jnp.bfloat16)
    extras = jnp.where(
        extra_cols == 0,
        loss_weight[:, None],
        jnp.where(
            extra_cols == 1,
            label_hi[:, None],
            jnp.where(extra_cols == 2, label_lo[:, None], jnp.zeros((), jnp.bfloat16)),
        ),
    )
    packed = jnp.concatenate([hidden, extras], axis=1)
    send = jnp.dot(place_hot, packed, preferred_element_type=jnp.float32).astype(jnp.bfloat16)

    received = lax.all_to_all(to_groups(send), AXES, split_axis=0, concat_axis=0, tiled=True)

    self_index = lax.axis_index(AXES)
    owned_mask = (language_owner == self_index).astype(jnp.int32)
    blocks = jnp.sum(owned_mask[:, None] * language_blocks, axis=0)
    slab = head_weight.reshape(SB, BLOCK, features)
    candidates = jnp.take(slab, blocks, axis=0).reshape(LB * BLOCK, features)

    back, token_rows, grads = middle(received, candidates)
    returned = from_groups(lax.all_to_all(back, AXES, split_axis=0, concat_axis=0, tiled=True))

    block_hot = blocks[None, :] == jnp.arange(SB, dtype=jnp.int32)[:, None]
    listed = jnp.any(block_hot, axis=1)
    list_index = jnp.sum(
        jnp.where(block_hot, jnp.arange(LB, dtype=jnp.int32)[None, :], 0), axis=1
    )
    grads_by_block = grads.reshape(places, LB, BLOCK)
    expanded = jnp.where(
        listed[None, :, None],
        jnp.take(grads_by_block, list_index, axis=1),
        jnp.zeros((), jnp.bfloat16),
    ).reshape(places, SB * BLOCK)
    head_grad = lax.dot_general(
        expanded, token_rows[:, :features], (((0,), (0,)), ((), ())),
        preferred_element_type=jnp.float32,
    ).astype(jnp.bfloat16)

    hidden_grad = lax.dot_general(
        place_hot, returned[:, :features], (((0,), (0,)), ((), ())),
        preferred_element_type=jnp.float32,
    ).astype(jnp.bfloat16)
    token_loss = lax.dot_general(
        place_hot, returned[:, features:], (((0,), (0,)), ((), ())),
        preferred_element_type=jnp.float32,
    )[:, 0].astype(jnp.bfloat16)
    return (hidden_grad, token_loss, head_grad)


def solution(mesh):
    in_specs = (
        P(AXES, None),
        P(AXES, None),
        P(),
        P(),
        P(AXES, None),
        P(AXES),
        P(AXES),
    )
    out_specs = (P(AXES, None), P(AXES), P(AXES, None))
    return jax.shard_map(shards, mesh=mesh, in_specs=in_specs, out_specs=out_specs, check_vma=False)
```

```python
import jax
import jax.numpy as jnp
from jax import lax
from jax.experimental import pallas as pl
from jax.experimental.pallas import tpu as pltpu
from jax.sharding import PartitionSpec as P

D = 2048
BLOCK = 128
SB = 8
LB = 6
CAP = 4
EXTRA = 128
LABEL_SPLIT = 128

SMOOTH = 0.1
AXES = ("vocab", "fsdp")
GROUPS_PER_STEP = 64


def place_tokens(token_language, language_owner):
    language = token_language[:, 0]
    languages = language_owner.shape[0]
    matches = language[:, None] == jnp.arange(languages, dtype=jnp.int32)[None, :]
    slot_ids = jnp.sum(jnp.where(matches, language_owner[None, :], 0), axis=1)
    positions = jnp.arange(language.shape[0], dtype=jnp.int32)
    earlier = (language[:, None] == language[None, :]) & (positions[None, :] < positions[:, None])
    rank_in_group = jnp.sum(earlier.astype(jnp.int32), axis=1)
    return slot_ids * CAP + rank_in_group


def _place(target_ref, hidden_ref, extras_ref, o_ref):
    step_rows = o_ref.shape[0] * o_ref.shape[1]
    tokens = hidden_ref.shape[0]
    first = pl.program_id(0) * step_rows
    hot = (
        lax.broadcasted_iota(jnp.int32, (step_rows, tokens), 0) + first == target_ref[...]
    ).astype(jnp.bfloat16)
    rows = jnp.dot(hot, hidden_ref[...], preferred_element_type=jnp.float32)
    extra = jnp.dot(hot, extras_ref[...], preferred_element_type=jnp.float32)
    out = jnp.concatenate([rows.astype(jnp.bfloat16), extra.astype(jnp.bfloat16)], axis=1)
    o_ref[...] = out.reshape(o_ref.shape)


def place(target_place, hidden, extras, groups):
    tokens, features = hidden.shape
    width = features + extras.shape[1]
    step = min(GROUPS_PER_STEP, groups)
    return pl.pallas_call(
        _place,
        grid=(groups // step,),
        in_specs=[
            pl.BlockSpec((1, tokens), lambda i: (0, 0)),
            pl.BlockSpec((tokens, features), lambda i: (0, 0)),
            pl.BlockSpec((tokens, extras.shape[1]), lambda i: (0, 0)),
        ],
        out_specs=pl.BlockSpec((step, CAP, width), lambda i: (i, 0, 0)),
        out_shape=jax.ShapeDtypeStruct((groups, CAP, width), hidden.dtype),
    )(target_place.reshape(1, tokens), hidden, extras)


def _unplace(target_ref, r_ref, rows_ref, extra_ref, acc_ref):
    i = pl.program_id(0)
    x = r_ref[...]
    x = x.reshape(x.shape[0] * x.shape[1], x.shape[2])
    step_rows = x.shape[0]
    tokens = target_ref.shape[0]
    hot = (
        lax.broadcasted_iota(jnp.int32, (tokens, step_rows), 1) + i * step_rows == target_ref[...]
    ).astype(jnp.bfloat16)
    part = jnp.dot(hot, x, preferred_element_type=jnp.float32)

    @pl.when(i == 0)
    def _():
        acc_ref[...] = part

    @pl.when(i > 0)
    def _():
        acc_ref[...] = acc_ref[...] + part

    @pl.when(i == pl.num_programs(0) - 1)
    def _():
        features = rows_ref.shape[1]
        total = acc_ref[...]
        rows_ref[...] = total[:, :features].astype(rows_ref.dtype)
        extra_ref[...] = total[:, features:].astype(extra_ref.dtype)


def unplace(target_place, returned, features):
    groups, cap, width = returned.shape
    tokens = target_place.shape[0]
    step = min(GROUPS_PER_STEP, groups)
    return pl.pallas_call(
        _unplace,
        grid=(groups // step,),
        in_specs=[
            pl.BlockSpec((tokens, 1), lambda i: (0, 0)),
            pl.BlockSpec((step, cap, width), lambda i: (i, 0, 0)),
        ],
        out_specs=[
            pl.BlockSpec((tokens, features), lambda i: (0, 0)),
            pl.BlockSpec((tokens, width - features), lambda i: (0, 0)),
        ],
        out_shape=[
            jax.ShapeDtypeStruct((tokens, features), returned.dtype),
            jax.ShapeDtypeStruct((tokens, width - features), returned.dtype),
        ],
        scratch_shapes=[pltpu.VMEM((tokens, width), jnp.float32)],
    )(target_place.reshape(tokens, 1), returned)


def _middle(r_ref, cand_ref, back_ref, rows_ref, grads_ref):
    x = r_ref[...]
    x = x.reshape(x.shape[0] * x.shape[1], x.shape[2])
    rows_ref[...] = x
    n, width = x.shape
    cand = cand_ref[...]
    columns, features = cand.shape
    logits = lax.dot_general(
        x[:, :features], cand, (((1,), (1,)), ((), ())), preferred_element_type=jnp.float32
    )
    weights = x[:, features : features + 1].astype(jnp.float32)
    targets = (
        x[:, features + 1 : features + 2].astype(jnp.float32) * LABEL_SPLIT
        + x[:, features + 2 : features + 3].astype(jnp.float32)
    ).astype(jnp.int32)
    row_max = jnp.max(logits, axis=1, keepdims=True)
    shifted = logits - row_max
    log_probs = shifted - jnp.log(jnp.sum(jnp.exp(shifted), axis=1, keepdims=True))
    onehot = (lax.broadcasted_iota(jnp.int32, logits.shape, 1) == targets).astype(jnp.float32)
    losses = -(1.0 - SMOOTH) * jnp.sum(onehot * log_probs, axis=1, keepdims=True) - (
        SMOOTH / columns
    ) * jnp.sum(log_probs, axis=1, keepdims=True)
    grads = (
        weights * (jnp.exp(log_probs) - (1.0 - SMOOTH) * onehot - SMOOTH / columns)
    ).astype(jnp.bfloat16)
    grads_ref[...] = grads
    row_grads = jnp.dot(grads, cand, preferred_element_type=jnp.float32).astype(jnp.bfloat16)
    extras = jnp.where(
        lax.broadcasted_iota(jnp.int32, (n, width - features), 1) == 0,
        losses.astype(jnp.bfloat16),
        jnp.zeros((), jnp.bfloat16),
    )
    back = jnp.concatenate([row_grads, extras], axis=1)
    back_ref[...] = back.reshape(back_ref.shape)


def middle(received, candidates):
    groups, cap, width = received.shape
    columns, features = candidates.shape
    step = min(GROUPS_PER_STEP, groups)
    return pl.pallas_call(
        _middle,
        grid=(groups // step,),
        in_specs=[
            pl.BlockSpec((step, cap, width), lambda i: (i, 0, 0)),
            pl.BlockSpec((columns, features), lambda i: (0, 0)),
        ],
        out_specs=[
            pl.BlockSpec((step, cap, width), lambda i: (i, 0, 0)),
            pl.BlockSpec((step * cap, width), lambda i: (i, 0)),
            pl.BlockSpec((step * cap, columns), lambda i: (i, 0)),
        ],
        out_shape=[
            jax.ShapeDtypeStruct((groups, cap, width), received.dtype),
            jax.ShapeDtypeStruct((groups * cap, width), received.dtype),
            jax.ShapeDtypeStruct((groups * cap, columns), jnp.bfloat16),
        ],
    )(received, candidates)


def shards(
    hidden, head_weight, language_blocks, language_owner, token_language, labels, loss_weight
):
    devices = lax.axis_size(AXES)
    tokens, features = hidden.shape
    places = devices * CAP
    assert head_weight.shape[0] == SB * BLOCK

    target_place = place_tokens(token_language, language_owner)
    extra_cols = lax.broadcasted_iota(jnp.int32, (tokens, EXTRA), 1)
    label_hi = (labels // LABEL_SPLIT).astype(jnp.bfloat16)
    label_lo = (labels % LABEL_SPLIT).astype(jnp.bfloat16)
    extras = jnp.where(
        extra_cols == 0,
        loss_weight[:, None],
        jnp.where(
            extra_cols == 1,
            label_hi[:, None],
            jnp.where(extra_cols == 2, label_lo[:, None], jnp.zeros((), jnp.bfloat16)),
        ),
    )
    send = place(target_place, hidden, extras, devices)
    received = lax.all_to_all(send, AXES, split_axis=0, concat_axis=0, tiled=True)

    self_index = lax.axis_index(AXES)
    owned_mask = (language_owner == self_index).astype(jnp.int32)
    blocks = jnp.sum(owned_mask[:, None] * language_blocks, axis=0)
    slab = head_weight.reshape(SB, BLOCK, features)
    candidates = jnp.take(slab, blocks, axis=0).reshape(LB * BLOCK, features)

    back, token_rows, grads = middle(received, candidates)
    returned = lax.all_to_all(back, AXES, split_axis=0, concat_axis=0, tiled=True)

    block_hot = blocks[None, :] == jnp.arange(SB, dtype=jnp.int32)[:, None]
    listed = jnp.any(block_hot, axis=1)
    list_index = jnp.sum(
        jnp.where(block_hot, jnp.arange(LB, dtype=jnp.int32)[None, :], 0), axis=1
    )
    grads_by_block = grads.reshape(places, LB, BLOCK)
    expanded = jnp.where(
        listed[None, :, None],
        jnp.take(grads_by_block, list_index, axis=1),
        jnp.zeros((), jnp.bfloat16),
    ).reshape(places, SB * BLOCK)
    head_grad = lax.dot_general(
        expanded, token_rows[:, :features], (((0,), (0,)), ((), ())),
        preferred_element_type=jnp.float32,
    ).astype(jnp.bfloat16)

    hidden_grad, returned_extras = unplace(target_place, returned, features)
    token_loss = returned_extras[:, 0]
    return (hidden_grad, token_loss, head_grad)


def solution(mesh):
    in_specs = (
        P(AXES, None),
        P(AXES, None),
        P(),
        P(),
        P(AXES, None),
        P(AXES),
        P(AXES),
    )
    out_specs = (P(AXES, None), P(AXES), P(AXES, None))
    return jax.shard_map(shards, mesh=mesh, in_specs=in_specs, out_specs=out_specs, check_vma=False)
```

```python
import jax
import jax.numpy as jnp
from jax import lax
from jax.experimental import pallas as pl
from jax.sharding import PartitionSpec as P

D = 2048
BLOCK = 128
SB = 8
LB = 6
CAP = 4
EXTRA = 128
LABEL_SPLIT = 128

SMOOTH = 0.1
AXES = ("vocab", "fsdp")
GROUPS_PER_STEP = 32


def place_tokens(token_language, language_owner):
    language = token_language[:, 0]
    languages = language_owner.shape[0]
    matches = language[:, None] == jnp.arange(languages, dtype=jnp.int32)[None, :]
    slot_ids = jnp.sum(jnp.where(matches, language_owner[None, :], 0), axis=1)
    positions = jnp.arange(language.shape[0], dtype=jnp.int32)
    earlier = (language[:, None] == language[None, :]) & (positions[None, :] < positions[:, None])
    rank_in_group = jnp.sum(earlier.astype(jnp.int32), axis=1)
    return slot_ids * CAP + rank_in_group


def _place(target_ref, hidden_ref, extras_ref, o_ref):
    step_rows = o_ref.shape[0] * o_ref.shape[1]
    tokens = hidden_ref.shape[0]
    first = pl.program_id(0) * step_rows
    hot = (
        lax.broadcasted_iota(jnp.int32, (step_rows, tokens), 0) + first == target_ref[...]
    ).astype(jnp.bfloat16)
    rows = jnp.dot(hot, hidden_ref[...], preferred_element_type=jnp.float32)
    extra = jnp.dot(hot, extras_ref[...], preferred_element_type=jnp.float32)
    out = jnp.concatenate([rows.astype(jnp.bfloat16), extra.astype(jnp.bfloat16)], axis=1)
    o_ref[...] = out.reshape(o_ref.shape)


def place(target_place, hidden, extras, groups):
    tokens, features = hidden.shape
    width = features + extras.shape[1]
    step = min(GROUPS_PER_STEP, groups)
    return pl.pallas_call(
        _place,
        grid=(groups // step,),
        in_specs=[
            pl.BlockSpec((1, tokens), lambda i: (0, 0)),
            pl.BlockSpec((tokens, features), lambda i: (0, 0)),
            pl.BlockSpec((tokens, extras.shape[1]), lambda i: (0, 0)),
        ],
        out_specs=pl.BlockSpec((step, CAP, width), lambda i: (i, 0, 0)),
        out_shape=jax.ShapeDtypeStruct((groups, CAP, width), hidden.dtype),
    )(target_place.reshape(1, tokens), hidden, extras)


def _unplace(target_ref, r_ref, rows_ref, extra_ref):
    x = r_ref[...]
    x = x.reshape(x.shape[0] * x.shape[1], x.shape[2])
    tokens = target_ref.shape[0]
    hot = (
        lax.broadcasted_iota(jnp.int32, (tokens, x.shape[0]), 1) == target_ref[...]
    ).astype(jnp.bfloat16)
    total = jnp.dot(hot, x, preferred_element_type=jnp.float32)
    features = rows_ref.shape[1]
    rows_ref[...] = total[:, :features].astype(rows_ref.dtype)
    extra_ref[...] = total[:, features:].astype(extra_ref.dtype)


def unplace(target_place, returned, features):
    groups, cap, width = returned.shape
    tokens = target_place.shape[0]
    return pl.pallas_call(
        _unplace,
        grid=(1,),
        in_specs=[
            pl.BlockSpec((tokens, 1), lambda i: (0, 0)),
            pl.BlockSpec((groups, cap, width), lambda i: (0, 0, 0)),
        ],
        out_specs=[
            pl.BlockSpec((tokens, features), lambda i: (0, 0)),
            pl.BlockSpec((tokens, width - features), lambda i: (0, 0)),
        ],
        out_shape=[
            jax.ShapeDtypeStruct((tokens, features), returned.dtype),
            jax.ShapeDtypeStruct((tokens, width - features), returned.dtype),
        ],
    )(target_place.reshape(tokens, 1), returned)


def _middle(r_ref, cand_ref, back_ref, rows_ref, grads_ref):
    x = r_ref[...]
    x = x.reshape(x.shape[0] * x.shape[1], x.shape[2])
    rows_ref[...] = x
    n, width = x.shape
    cand = cand_ref[...]
    columns, features = cand.shape
    logits = lax.dot_general(
        x[:, :features], cand, (((1,), (1,)), ((), ())), preferred_element_type=jnp.float32
    )
    weights = x[:, features : features + 1].astype(jnp.float32)
    targets = (
        x[:, features + 1 : features + 2].astype(jnp.float32) * LABEL_SPLIT
        + x[:, features + 2 : features + 3].astype(jnp.float32)
    ).astype(jnp.int32)
    row_max = jnp.max(logits, axis=1, keepdims=True)
    shifted = logits - row_max
    log_probs = shifted - jnp.log(jnp.sum(jnp.exp(shifted), axis=1, keepdims=True))
    onehot = (lax.broadcasted_iota(jnp.int32, logits.shape, 1) == targets).astype(jnp.float32)
    losses = -(1.0 - SMOOTH) * jnp.sum(onehot * log_probs, axis=1, keepdims=True) - (
        SMOOTH / columns
    ) * jnp.sum(log_probs, axis=1, keepdims=True)
    grads = (
        weights * (jnp.exp(log_probs) - (1.0 - SMOOTH) * onehot - SMOOTH / columns)
    ).astype(jnp.bfloat16)
    grads_ref[...] = grads
    row_grads = jnp.dot(grads, cand, preferred_element_type=jnp.float32).astype(jnp.bfloat16)
    extras = jnp.where(
        lax.broadcasted_iota(jnp.int32, (n, width - features), 1) == 0,
        losses.astype(jnp.bfloat16),
        jnp.zeros((), jnp.bfloat16),
    )
    back = jnp.concatenate([row_grads, extras], axis=1)
    back_ref[...] = back.reshape(back_ref.shape)


def middle(received, candidates):
    groups, cap, width = received.shape
    columns, features = candidates.shape
    step = min(GROUPS_PER_STEP, groups)
    return pl.pallas_call(
        _middle,
        grid=(groups // step,),
        in_specs=[
            pl.BlockSpec((step, cap, width), lambda i: (i, 0, 0)),
            pl.BlockSpec((columns, features), lambda i: (0, 0)),
        ],
        out_specs=[
            pl.BlockSpec((step, cap, width), lambda i: (i, 0, 0)),
            pl.BlockSpec((step * cap, width), lambda i: (i, 0)),
            pl.BlockSpec((step * cap, columns), lambda i: (i, 0)),
        ],
        out_shape=[
            jax.ShapeDtypeStruct((groups, cap, width), received.dtype),
            jax.ShapeDtypeStruct((groups * cap, width), received.dtype),
            jax.ShapeDtypeStruct((groups * cap, columns), jnp.bfloat16),
        ],
    )(received, candidates)


def shards(
    hidden, head_weight, language_blocks, language_owner, token_language, labels, loss_weight
):
    devices = lax.axis_size(AXES)
    tokens, features = hidden.shape
    places = devices * CAP
    assert head_weight.shape[0] == SB * BLOCK

    target_place = place_tokens(token_language, language_owner)
    extra_cols = lax.broadcasted_iota(jnp.int32, (tokens, EXTRA), 1)
    label_hi = (labels // LABEL_SPLIT).astype(jnp.bfloat16)
    label_lo = (labels % LABEL_SPLIT).astype(jnp.bfloat16)
    extras = jnp.where(
        extra_cols == 0,
        loss_weight[:, None],
        jnp.where(
            extra_cols == 1,
            label_hi[:, None],
            jnp.where(extra_cols == 2, label_lo[:, None], jnp.zeros((), jnp.bfloat16)),
        ),
    )
    send = place(target_place, hidden, extras, devices)
    received = lax.all_to_all(send, AXES, split_axis=0, concat_axis=0, tiled=True)

    self_index = lax.axis_index(AXES)
    owned_mask = (language_owner == self_index).astype(jnp.int32)
    blocks = jnp.sum(owned_mask[:, None] * language_blocks, axis=0)
    slab = head_weight.reshape(SB, BLOCK, features)
    candidates = jnp.take(slab, blocks, axis=0).reshape(LB * BLOCK, features)

    back, token_rows, grads = middle(received, candidates)
    returned = lax.all_to_all(back, AXES, split_axis=0, concat_axis=0, tiled=True)

    block_hot = blocks[None, :] == jnp.arange(SB, dtype=jnp.int32)[:, None]
    listed = jnp.any(block_hot, axis=1)
    list_index = jnp.sum(
        jnp.where(block_hot, jnp.arange(LB, dtype=jnp.int32)[None, :], 0), axis=1
    )
    grads_by_block = grads.reshape(places, LB, BLOCK)
    expanded = jnp.where(
        listed[None, :, None],
        jnp.take(grads_by_block, list_index, axis=1),
        jnp.zeros((), jnp.bfloat16),
    ).reshape(places, SB * BLOCK)
    head_grad = lax.dot_general(
        expanded, token_rows[:, :features], (((0,), (0,)), ((), ())),
        preferred_element_type=jnp.float32,
    ).astype(jnp.bfloat16)

    hidden_grad, returned_extras = unplace(target_place, returned, features)
    token_loss = returned_extras[:, 0]
    return (hidden_grad, token_loss, head_grad)


def solution(mesh):
    in_specs = (
        P(AXES, None),
        P(AXES, None),
        P(),
        P(),
        P(AXES, None),
        P(AXES),
        P(AXES),
    )
    out_specs = (P(AXES, None), P(AXES), P(AXES, None))
    return jax.shard_map(shards, mesh=mesh, in_specs=in_specs, out_specs=out_specs, check_vma=False)
```

```python
import jax
import jax.numpy as jnp
from jax import lax
from jax.experimental import pallas as pl
from jax.sharding import PartitionSpec as P

D = 2048
BLOCK = 128
SB = 8
LB = 6
CAP = 4
EXTRA = 128
LABEL_SPLIT = 128

SMOOTH = 0.1
AXES = ("vocab", "fsdp")
GROUPS_PER_STEP = 128


def place_tokens(token_language, language_owner):
    language = token_language[:, 0]
    languages = language_owner.shape[0]
    matches = language[:, None] == jnp.arange(languages, dtype=jnp.int32)[None, :]
    slot_ids = jnp.sum(jnp.where(matches, language_owner[None, :], 0), axis=1)
    positions = jnp.arange(language.shape[0], dtype=jnp.int32)
    earlier = (language[:, None] == language[None, :]) & (positions[None, :] < positions[:, None])
    rank_in_group = jnp.sum(earlier.astype(jnp.int32), axis=1)
    return slot_ids * CAP + rank_in_group


def _place(target_ref, hidden_ref, extras_ref, o_ref):
    step_rows = o_ref.shape[0] * o_ref.shape[1]
    tokens = hidden_ref.shape[0]
    first = pl.program_id(0) * step_rows
    hot = (
        lax.broadcasted_iota(jnp.int32, (step_rows, tokens), 0) + first == target_ref[...]
    ).astype(jnp.bfloat16)
    rows = jnp.dot(hot, hidden_ref[...], preferred_element_type=jnp.float32)
    extra = jnp.dot(hot, extras_ref[...], preferred_element_type=jnp.float32)
    out = jnp.concatenate([rows.astype(jnp.bfloat16), extra.astype(jnp.bfloat16)], axis=1)
    o_ref[...] = out.reshape(o_ref.shape)


def place(target_place, hidden, extras, groups):
    tokens, features = hidden.shape
    width = features + extras.shape[1]
    step = min(GROUPS_PER_STEP, groups)
    return pl.pallas_call(
        _place,
        grid=(groups // step,),
        in_specs=[
            pl.BlockSpec((1, tokens), lambda i: (0, 0)),
            pl.BlockSpec((tokens, features), lambda i: (0, 0)),
            pl.BlockSpec((tokens, extras.shape[1]), lambda i: (0, 0)),
        ],
        out_specs=pl.BlockSpec((step, CAP, width), lambda i: (i, 0, 0)),
        out_shape=jax.ShapeDtypeStruct((groups, CAP, width), hidden.dtype),
    )(target_place.reshape(1, tokens), hidden, extras)


def _unplace(target_ref, r_ref, rows_ref, extra_ref):
    x = r_ref[...]
    x = x.reshape(x.shape[0] * x.shape[1], x.shape[2])
    tokens = target_ref.shape[0]
    hot = (
        lax.broadcasted_iota(jnp.int32, (tokens, x.shape[0]), 1) == target_ref[...]
    ).astype(jnp.bfloat16)
    total = jnp.dot(hot, x, preferred_element_type=jnp.float32)
    features = rows_ref.shape[1]
    rows_ref[...] = total[:, :features].astype(rows_ref.dtype)
    extra_ref[...] = total[:, features:].astype(extra_ref.dtype)


def unplace(target_place, returned, features):
    groups, cap, width = returned.shape
    tokens = target_place.shape[0]
    return pl.pallas_call(
        _unplace,
        grid=(1,),
        in_specs=[
            pl.BlockSpec((tokens, 1), lambda i: (0, 0)),
            pl.BlockSpec((groups, cap, width), lambda i: (0, 0, 0)),
        ],
        out_specs=[
            pl.BlockSpec((tokens, features), lambda i: (0, 0)),
            pl.BlockSpec((tokens, width - features), lambda i: (0, 0)),
        ],
        out_shape=[
            jax.ShapeDtypeStruct((tokens, features), returned.dtype),
            jax.ShapeDtypeStruct((tokens, width - features), returned.dtype),
        ],
    )(target_place.reshape(tokens, 1), returned)


def _middle(r_ref, cand_ref, back_ref, rows_ref, grads_ref):
    x = r_ref[...]
    x = x.reshape(x.shape[0] * x.shape[1], x.shape[2])
    rows_ref[...] = x
    n, width = x.shape
    cand = cand_ref[...]
    columns, features = cand.shape
    logits = lax.dot_general(
        x[:, :features], cand, (((1,), (1,)), ((), ())), preferred_element_type=jnp.float32
    )
    weights = x[:, features : features + 1].astype(jnp.float32)
    targets = (
        x[:, features + 1 : features + 2].astype(jnp.float32) * LABEL_SPLIT
        + x[:, features + 2 : features + 3].astype(jnp.float32)
    ).astype(jnp.int32)
    row_max = jnp.max(logits, axis=1, keepdims=True)
    shifted = logits - row_max
    log_probs = shifted - jnp.log(jnp.sum(jnp.exp(shifted), axis=1, keepdims=True))
    onehot = (lax.broadcasted_iota(jnp.int32, logits.shape, 1) == targets).astype(jnp.float32)
    losses = -(1.0 - SMOOTH) * jnp.sum(onehot * log_probs, axis=1, keepdims=True) - (
        SMOOTH / columns
    ) * jnp.sum(log_probs, axis=1, keepdims=True)
    grads = (
        weights * (jnp.exp(log_probs) - (1.0 - SMOOTH) * onehot - SMOOTH / columns)
    ).astype(jnp.bfloat16)
    grads_ref[...] = grads
    row_grads = jnp.dot(grads, cand, preferred_element_type=jnp.float32).astype(jnp.bfloat16)
    extras = jnp.where(
        lax.broadcasted_iota(jnp.int32, (n, width - features), 1) == 0,
        losses.astype(jnp.bfloat16),
        jnp.zeros((), jnp.bfloat16),
    )
    back = jnp.concatenate([row_grads, extras], axis=1)
    back_ref[...] = back.reshape(back_ref.shape)


def middle(received, candidates):
    groups, cap, width = received.shape
    columns, features = candidates.shape
    step = min(GROUPS_PER_STEP, groups)
    return pl.pallas_call(
        _middle,
        grid=(groups // step,),
        in_specs=[
            pl.BlockSpec((step, cap, width), lambda i: (i, 0, 0)),
            pl.BlockSpec((columns, features), lambda i: (0, 0)),
        ],
        out_specs=[
            pl.BlockSpec((step, cap, width), lambda i: (i, 0, 0)),
            pl.BlockSpec((step * cap, width), lambda i: (i, 0)),
            pl.BlockSpec((step * cap, columns), lambda i: (i, 0)),
        ],
        out_shape=[
            jax.ShapeDtypeStruct((groups, cap, width), received.dtype),
            jax.ShapeDtypeStruct((groups * cap, width), received.dtype),
            jax.ShapeDtypeStruct((groups * cap, columns), jnp.bfloat16),
        ],
    )(received, candidates)


def shards(
    hidden, head_weight, language_blocks, language_owner, token_language, labels, loss_weight
):
    devices = lax.axis_size(AXES)
    tokens, features = hidden.shape
    places = devices * CAP
    assert head_weight.shape[0] == SB * BLOCK

    target_place = place_tokens(token_language, language_owner)
    extra_cols = lax.broadcasted_iota(jnp.int32, (tokens, EXTRA), 1)
    label_hi = (labels // LABEL_SPLIT).astype(jnp.bfloat16)
    label_lo = (labels % LABEL_SPLIT).astype(jnp.bfloat16)
    extras = jnp.where(
        extra_cols == 0,
        loss_weight[:, None],
        jnp.where(
            extra_cols == 1,
            label_hi[:, None],
            jnp.where(extra_cols == 2, label_lo[:, None], jnp.zeros((), jnp.bfloat16)),
        ),
    )
    send = place(target_place, hidden, extras, devices)
    received = lax.all_to_all(send, AXES, split_axis=0, concat_axis=0, tiled=True)

    self_index = lax.axis_index(AXES)
    owned_mask = (language_owner == self_index).astype(jnp.int32)
    blocks = jnp.sum(owned_mask[:, None] * language_blocks, axis=0)
    slab = head_weight.reshape(SB, BLOCK, features)
    candidates = jnp.take(slab, blocks, axis=0).reshape(LB * BLOCK, features)

    back, token_rows, grads = middle(received, candidates)
    returned = lax.all_to_all(back, AXES, split_axis=0, concat_axis=0, tiled=True)

    block_hot = blocks[None, :] == jnp.arange(SB, dtype=jnp.int32)[:, None]
    listed = jnp.any(block_hot, axis=1)
    list_index = jnp.sum(
        jnp.where(block_hot, jnp.arange(LB, dtype=jnp.int32)[None, :], 0), axis=1
    )
    grads_by_block = grads.reshape(places, LB, BLOCK)
    expanded = jnp.where(
        listed[None, :, None],
        jnp.take(grads_by_block, list_index, axis=1),
        jnp.zeros((), jnp.bfloat16),
    ).reshape(places, SB * BLOCK)
    head_grad = lax.dot_general(
        expanded, token_rows[:, :features], (((0,), (0,)), ((), ())),
        preferred_element_type=jnp.float32,
    ).astype(jnp.bfloat16)

    hidden_grad, returned_extras = unplace(target_place, returned, features)
    token_loss = returned_extras[:, 0]
    return (hidden_grad, token_loss, head_grad)


def solution(mesh):
    in_specs = (
        P(AXES, None),
        P(AXES, None),
        P(),
        P(),
        P(AXES, None),
        P(AXES),
        P(AXES),
    )
    out_specs = (P(AXES, None), P(AXES), P(AXES, None))
    return jax.shard_map(shards, mesh=mesh, in_specs=in_specs, out_specs=out_specs, check_vma=False)
```

```python
import jax
import jax.numpy as jnp
from jax import lax
from jax.experimental import pallas as pl
from jax.sharding import PartitionSpec as P

D = 2048
BLOCK = 128
SB = 8
LB = 6
CAP = 4
EXTRA = 128
LABEL_SPLIT = 128

SMOOTH = 0.1
AXES = ("vocab", "fsdp")
GROUPS_PER_STEP = 128


def _place(lang_col_ref, lang_row_ref, owner_ref, labels_ref, weights_ref, hidden_ref, o_ref, target_ref):
    tokens = hidden_ref.shape[0]
    languages = owner_ref.shape[0]
    lang_row = lang_row_ref[...]
    earlier = (lang_col_ref[...] == lang_row) & (
        lax.broadcasted_iota(jnp.int32, (tokens, tokens), 0)
        < lax.broadcasted_iota(jnp.int32, (tokens, tokens), 1)
    )
    rank = jnp.sum(earlier.astype(jnp.int32), axis=0, keepdims=True)
    slot = jnp.sum(
        jnp.where(
            lax.broadcasted_iota(jnp.int32, (languages, tokens), 0) == lang_row, owner_ref[...], 0
        ),
        axis=0,
        keepdims=True,
    )
    target = slot * CAP + rank
    target_ref[...] = target
    labels = labels_ref[...]
    kind = lax.broadcasted_iota(jnp.int32, (EXTRA, tokens), 0)
    extras_t = jnp.where(
        kind == 0,
        weights_ref[...].astype(jnp.float32),
        jnp.where(
            kind == 1,
            (labels // LABEL_SPLIT).astype(jnp.float32),
            jnp.where(kind == 2, (labels % LABEL_SPLIT).astype(jnp.float32), 0.0),
        ),
    ).astype(jnp.bfloat16)
    step_rows = o_ref.shape[0] * o_ref.shape[1]
    first = pl.program_id(0) * step_rows
    hot = (lax.broadcasted_iota(jnp.int32, (step_rows, tokens), 0) + first == target).astype(
        jnp.bfloat16
    )
    rows = jnp.dot(hot, hidden_ref[...], preferred_element_type=jnp.float32)
    extra = lax.dot_general(
        hot, extras_t, (((1,), (1,)), ((), ())), preferred_element_type=jnp.float32
    )
    out = jnp.concatenate([rows.astype(jnp.bfloat16), extra.astype(jnp.bfloat16)], axis=1)
    o_ref[...] = out.reshape(o_ref.shape)


def place(token_language, language_owner, labels, loss_weight, hidden, groups):
    tokens, features = hidden.shape
    languages = language_owner.shape[0]
    width = features + EXTRA
    step = min(GROUPS_PER_STEP, groups)
    whole = lambda i: (0, 0)
    return pl.pallas_call(
        _place,
        grid=(groups // step,),
        in_specs=[
            pl.BlockSpec((tokens, 1), whole),
            pl.BlockSpec((1, tokens), whole),
            pl.BlockSpec((languages, 1), whole),
            pl.BlockSpec((1, tokens), whole),
            pl.BlockSpec((1, tokens), whole),
            pl.BlockSpec((tokens, features), whole),
        ],
        out_specs=[
            pl.BlockSpec((step, CAP, width), lambda i: (i, 0, 0)),
            pl.BlockSpec((1, tokens), whole),
        ],
        out_shape=[
            jax.ShapeDtypeStruct((groups, CAP, width), hidden.dtype),
            jax.ShapeDtypeStruct((1, tokens), jnp.int32),
        ],
    )(
        token_language,
        token_language.reshape(1, tokens),
        language_owner.reshape(languages, 1),
        labels.reshape(1, tokens),
        loss_weight.reshape(1, tokens),
        hidden,
    )


def _unplace(target_ref, r_ref, rows_ref, loss_ref):
    x = r_ref[...]
    x = x.reshape(x.shape[0] * x.shape[1], x.shape[2])
    tokens = target_ref.shape[1]
    features = rows_ref.shape[1]
    hot_t = (lax.broadcasted_iota(jnp.int32, (x.shape[0], tokens), 0) == target_ref[...]).astype(
        jnp.bfloat16
    )
    rows = lax.dot_general(
        hot_t, x[:, :features], (((0,), (0,)), ((), ())), preferred_element_type=jnp.float32
    )
    rows_ref[...] = rows.astype(rows_ref.dtype)
    loss = lax.dot_general(
        x[:, features:], hot_t, (((0,), (0,)), ((), ())), preferred_element_type=jnp.float32
    )
    loss_ref[...] = loss[0:1, :].astype(loss_ref.dtype)


def unplace(target_row, returned, features):
    groups, cap, width = returned.shape
    tokens = target_row.shape[1]
    return pl.pallas_call(
        _unplace,
        grid=(1,),
        in_specs=[
            pl.BlockSpec((1, tokens), lambda i: (0, 0)),
            pl.BlockSpec((groups, cap, width), lambda i: (0, 0, 0)),
        ],
        out_specs=[
            pl.BlockSpec((tokens, features), lambda i: (0, 0)),
            pl.BlockSpec((1, tokens), lambda i: (0, 0)),
        ],
        out_shape=[
            jax.ShapeDtypeStruct((tokens, features), returned.dtype),
            jax.ShapeDtypeStruct((1, tokens), returned.dtype),
        ],
    )(target_row, returned)


def _middle(r_ref, cand_ref, back_ref, rows_ref, grads_ref):
    x = r_ref[...]
    x = x.reshape(x.shape[0] * x.shape[1], x.shape[2])
    rows_ref[...] = x
    n, width = x.shape
    cand = cand_ref[...]
    columns, features = cand.shape
    logits = lax.dot_general(
        x[:, :features], cand, (((1,), (1,)), ((), ())), preferred_element_type=jnp.float32
    )
    weights = x[:, features : features + 1].astype(jnp.float32)
    targets = (
        x[:, features + 1 : features + 2].astype(jnp.float32) * LABEL_SPLIT
        + x[:, features + 2 : features + 3].astype(jnp.float32)
    ).astype(jnp.int32)
    row_max = jnp.max(logits, axis=1, keepdims=True)
    shifted = logits - row_max
    exps = jnp.exp(shifted)
    total = jnp.sum(exps, axis=1, keepdims=True)
    log_probs = shifted - jnp.log(total)
    onehot = (lax.broadcasted_iota(jnp.int32, logits.shape, 1) == targets).astype(jnp.float32)
    losses = -(1.0 - SMOOTH) * jnp.sum(onehot * log_probs, axis=1, keepdims=True) - (
        SMOOTH / columns
    ) * jnp.sum(log_probs, axis=1, keepdims=True)
    probs = exps * (1.0 / total)
    grads = (weights * (probs - (1.0 - SMOOTH) * onehot - SMOOTH / columns)).astype(jnp.bfloat16)
    grads_ref[...] = grads
    row_grads = jnp.dot(grads, cand, preferred_element_type=jnp.float32).astype(jnp.bfloat16)
    extras = jnp.where(
        lax.broadcasted_iota(jnp.int32, (n, width - features), 1) == 0,
        losses.astype(jnp.bfloat16),
        jnp.zeros((), jnp.bfloat16),
    )
    back = jnp.concatenate([row_grads, extras], axis=1)
    back_ref[...] = back.reshape(back_ref.shape)


def middle(received, candidates):
    groups, cap, width = received.shape
    columns, features = candidates.shape
    step = min(GROUPS_PER_STEP, groups)
    return pl.pallas_call(
        _middle,
        grid=(groups // step,),
        in_specs=[
            pl.BlockSpec((step, cap, width), lambda i: (i, 0, 0)),
            pl.BlockSpec((columns, features), lambda i: (0, 0)),
        ],
        out_specs=[
            pl.BlockSpec((step, cap, width), lambda i: (i, 0, 0)),
            pl.BlockSpec((step * cap, width), lambda i: (i, 0)),
            pl.BlockSpec((step * cap, columns), lambda i: (i, 0)),
        ],
        out_shape=[
            jax.ShapeDtypeStruct((groups, cap, width), received.dtype),
            jax.ShapeDtypeStruct((groups * cap, width), received.dtype),
            jax.ShapeDtypeStruct((groups * cap, columns), jnp.bfloat16),
        ],
    )(received, candidates)


def shards(
    hidden, head_weight, language_blocks, language_owner, token_language, labels, loss_weight
):
    devices = lax.axis_size(AXES)
    tokens, features = hidden.shape
    places = devices * CAP
    assert head_weight.shape[0] == SB * BLOCK

    send, target_row = place(token_language, language_owner, labels, loss_weight, hidden, devices)
    received = lax.all_to_all(send, AXES, split_axis=0, concat_axis=0, tiled=True)

    self_index = lax.axis_index(AXES)
    owned_mask = (language_owner == self_index).astype(jnp.int32)
    blocks = jnp.sum(owned_mask[:, None] * language_blocks, axis=0)
    slab = head_weight.reshape(SB, BLOCK, features)
    candidates = jnp.take(slab, blocks, axis=0).reshape(LB * BLOCK, features)

    back, token_rows, grads = middle(received, candidates)
    returned = lax.all_to_all(back, AXES, split_axis=0, concat_axis=0, tiled=True)

    block_hot = blocks[None, :] == jnp.arange(SB, dtype=jnp.int32)[:, None]
    listed = jnp.any(block_hot, axis=1)
    list_index = jnp.sum(
        jnp.where(block_hot, jnp.arange(LB, dtype=jnp.int32)[None, :], 0), axis=1
    )
    grads_by_block = grads.reshape(places, LB, BLOCK)
    expanded = jnp.where(
        listed[None, :, None],
        jnp.take(grads_by_block, list_index, axis=1),
        jnp.zeros((), jnp.bfloat16),
    ).reshape(places, SB * BLOCK)
    head_grad = lax.dot_general(
        expanded, token_rows[:, :features], (((0,), (0,)), ((), ())),
        preferred_element_type=jnp.float32,
    ).astype(jnp.bfloat16)

    hidden_grad, loss_row = unplace(target_row, returned, features)
    token_loss = loss_row.reshape(tokens)
    return (hidden_grad, token_loss, head_grad)


def solution(mesh):
    in_specs = (
        P(AXES, None),
        P(AXES, None),
        P(),
        P(),
        P(AXES, None),
        P(AXES),
        P(AXES),
    )
    out_specs = (P(AXES, None), P(AXES), P(AXES, None))
    return jax.shard_map(shards, mesh=mesh, in_specs=in_specs, out_specs=out_specs, check_vma=False)
```

```python
import jax
import jax.numpy as jnp
from jax import lax
from jax.experimental import pallas as pl
from jax.sharding import PartitionSpec as P

D = 2048
BLOCK = 128
SB = 8
LB = 6
CAP = 4
EXTRA = 128
LABEL_SPLIT = 128

SMOOTH = 0.1
AXES = ("vocab", "fsdp")
GROUPS_PER_STEP = 128


def _place(lang_ref, owner_ref, labels_ref, weights_ref, hidden_ref, o_ref, target_ref):
    tokens = hidden_ref.shape[0]
    languages = owner_ref.shape[0]
    lang = lang_ref[...].reshape(1, tokens)
    owner = owner_ref[...].reshape(1, languages)
    is_lang = (lax.broadcasted_iota(jnp.int32, (languages, tokens), 0) == lang).astype(
        jnp.bfloat16
    )
    same = lax.dot_general(
        is_lang, is_lang, (((0,), (0,)), ((), ())), preferred_element_type=jnp.float32
    )
    before = lax.broadcasted_iota(jnp.int32, (tokens, tokens), 0) < lax.broadcasted_iota(
        jnp.int32, (tokens, tokens), 1
    )
    rank = jnp.sum(jnp.where(before, same, 0.0), axis=0, keepdims=True)
    slot = jnp.dot(owner.astype(jnp.bfloat16), is_lang, preferred_element_type=jnp.float32)
    target = (slot * CAP + rank).astype(jnp.int32)
    target_ref[...] = target
    labels = labels_ref[...].reshape(1, tokens)
    kind = lax.broadcasted_iota(jnp.int32, (EXTRA, tokens), 0)
    extras_t = jnp.where(
        kind == 0,
        weights_ref[...].reshape(1, tokens).astype(jnp.float32),
        jnp.where(
            kind == 1,
            (labels // LABEL_SPLIT).astype(jnp.float32),
            jnp.where(kind == 2, (labels % LABEL_SPLIT).astype(jnp.float32), 0.0),
        ),
    ).astype(jnp.bfloat16)
    step_rows = o_ref.shape[0] * o_ref.shape[1]
    first = pl.program_id(0) * step_rows
    hot = (lax.broadcasted_iota(jnp.int32, (step_rows, tokens), 0) + first == target).astype(
        jnp.bfloat16
    )
    rows = jnp.dot(hot, hidden_ref[...], preferred_element_type=jnp.float32)
    extra = lax.dot_general(
        hot, extras_t, (((1,), (1,)), ((), ())), preferred_element_type=jnp.float32
    )
    out = jnp.concatenate([rows.astype(jnp.bfloat16), extra.astype(jnp.bfloat16)], axis=1)
    o_ref[...] = out.reshape(o_ref.shape)


def place(token_language, language_owner, labels, loss_weight, hidden, groups):
    tokens, features = hidden.shape
    languages = language_owner.shape[0]
    width = features + EXTRA
    step = min(GROUPS_PER_STEP, groups)
    whole = lambda i: (0,)
    return pl.pallas_call(
        _place,
        grid=(groups // step,),
        in_specs=[
            pl.BlockSpec((tokens,), whole),
            pl.BlockSpec((languages,), whole),
            pl.BlockSpec((tokens,), whole),
            pl.BlockSpec((tokens,), whole),
            pl.BlockSpec((tokens, features), lambda i: (0, 0)),
        ],
        out_specs=[
            pl.BlockSpec((step, CAP, width), lambda i: (i, 0, 0)),
            pl.BlockSpec((1, tokens), lambda i: (0, 0)),
        ],
        out_shape=[
            jax.ShapeDtypeStruct((groups, CAP, width), hidden.dtype),
            jax.ShapeDtypeStruct((1, tokens), jnp.int32),
        ],
    )(token_language.reshape(tokens), language_owner, labels, loss_weight, hidden)


def _unplace(target_ref, r_ref, rows_ref, loss_ref):
    x = r_ref[...]
    x = x.reshape(x.shape[0] * x.shape[1], x.shape[2])
    tokens = target_ref.shape[1]
    features = rows_ref.shape[1]
    hot_t = (lax.broadcasted_iota(jnp.int32, (x.shape[0], tokens), 0) == target_ref[...]).astype(
        jnp.bfloat16
    )
    rows = lax.dot_general(
        hot_t, x[:, :features], (((0,), (0,)), ((), ())), preferred_element_type=jnp.float32
    )
    rows_ref[...] = rows.astype(rows_ref.dtype)
    loss = lax.dot_general(
        x[:, features:], hot_t, (((0,), (0,)), ((), ())), preferred_element_type=jnp.float32
    )
    loss_ref[...] = loss[0:1, :].astype(loss_ref.dtype).reshape(loss_ref.shape)


def unplace(target_row, returned, features):
    groups, cap, width = returned.shape
    tokens = target_row.shape[1]
    return pl.pallas_call(
        _unplace,
        grid=(1,),
        in_specs=[
            pl.BlockSpec((1, tokens), lambda i: (0, 0)),
            pl.BlockSpec((groups, cap, width), lambda i: (0, 0, 0)),
        ],
        out_specs=[
            pl.BlockSpec((tokens, features), lambda i: (0, 0)),
            pl.BlockSpec((tokens,), lambda i: (0,)),
        ],
        out_shape=[
            jax.ShapeDtypeStruct((tokens, features), returned.dtype),
            jax.ShapeDtypeStruct((tokens,), returned.dtype),
        ],
    )(target_row, returned)


def _middle(r_ref, cand_ref, back_ref, rows_ref, grads_ref):
    x = r_ref[...]
    x = x.reshape(x.shape[0] * x.shape[1], x.shape[2])
    rows_ref[...] = x
    n, width = x.shape
    cand = cand_ref[...]
    columns, features = cand.shape
    logits = lax.dot_general(
        x[:, :features], cand, (((1,), (1,)), ((), ())), preferred_element_type=jnp.float32
    )
    weights = x[:, features : features + 1].astype(jnp.float32)
    targets = (
        x[:, features + 1 : features + 2].astype(jnp.float32) * LABEL_SPLIT
        + x[:, features + 2 : features + 3].astype(jnp.float32)
    ).astype(jnp.int32)
    row_max = jnp.max(logits, axis=1, keepdims=True)
    shifted = logits - row_max
    exps = jnp.exp(shifted)
    total = jnp.sum(exps, axis=1, keepdims=True)
    log_probs = shifted - jnp.log(total)
    onehot = (lax.broadcasted_iota(jnp.int32, logits.shape, 1) == targets).astype(jnp.float32)
    losses = -(1.0 - SMOOTH) * jnp.sum(onehot * log_probs, axis=1, keepdims=True) - (
        SMOOTH / columns
    ) * jnp.sum(log_probs, axis=1, keepdims=True)
    probs = exps * (1.0 / total)
    grads = (weights * (probs - (1.0 - SMOOTH) * onehot - SMOOTH / columns)).astype(jnp.bfloat16)
    grads_ref[...] = grads
    row_grads = jnp.dot(grads, cand, preferred_element_type=jnp.float32).astype(jnp.bfloat16)
    extras = jnp.where(
        lax.broadcasted_iota(jnp.int32, (n, width - features), 1) == 0,
        losses.astype(jnp.bfloat16),
        jnp.zeros((), jnp.bfloat16),
    )
    back = jnp.concatenate([row_grads, extras], axis=1)
    back_ref[...] = back.reshape(back_ref.shape)


def middle(received, candidates):
    groups, cap, width = received.shape
    columns, features = candidates.shape
    step = min(GROUPS_PER_STEP, groups)
    return pl.pallas_call(
        _middle,
        grid=(groups // step,),
        in_specs=[
            pl.BlockSpec((step, cap, width), lambda i: (i, 0, 0)),
            pl.BlockSpec((columns, features), lambda i: (0, 0)),
        ],
        out_specs=[
            pl.BlockSpec((step, cap, width), lambda i: (i, 0, 0)),
            pl.BlockSpec((step * cap, width), lambda i: (i, 0)),
            pl.BlockSpec((step * cap, columns), lambda i: (i, 0)),
        ],
        out_shape=[
            jax.ShapeDtypeStruct((groups, cap, width), received.dtype),
            jax.ShapeDtypeStruct((groups * cap, width), received.dtype),
            jax.ShapeDtypeStruct((groups * cap, columns), jnp.bfloat16),
        ],
    )(received, candidates)


def shards(
    hidden, head_weight, language_blocks, language_owner, token_language, labels, loss_weight
):
    devices = lax.axis_size(AXES)
    tokens, features = hidden.shape
    places = devices * CAP
    assert head_weight.shape[0] == SB * BLOCK

    send, target_row = place(token_language, language_owner, labels, loss_weight, hidden, devices)
    received = lax.all_to_all(send, AXES, split_axis=0, concat_axis=0, tiled=True)

    self_index = lax.axis_index(AXES)
    owned_mask = (language_owner == self_index).astype(jnp.int32)
    blocks = jnp.sum(owned_mask[:, None] * language_blocks, axis=0)
    slab = head_weight.reshape(SB, BLOCK, features)
    candidates = jnp.take(slab, blocks, axis=0).reshape(LB * BLOCK, features)

    back, token_rows, grads = middle(received, candidates)
    returned = lax.all_to_all(back, AXES, split_axis=0, concat_axis=0, tiled=True)

    block_hot = blocks[None, :] == jnp.arange(SB, dtype=jnp.int32)[:, None]
    listed = jnp.any(block_hot, axis=1)
    list_index = jnp.sum(
        jnp.where(block_hot, jnp.arange(LB, dtype=jnp.int32)[None, :], 0), axis=1
    )
    grads_by_block = grads.reshape(places, LB, BLOCK)
    expanded = jnp.where(
        listed[None, :, None],
        jnp.take(grads_by_block, list_index, axis=1),
        jnp.zeros((), jnp.bfloat16),
    ).reshape(places, SB * BLOCK)
    head_grad = lax.dot_general(
        expanded, token_rows[:, :features], (((0,), (0,)), ((), ())),
        preferred_element_type=jnp.float32,
    ).astype(jnp.bfloat16)

    hidden_grad, token_loss = unplace(target_row, returned, features)
    return (hidden_grad, token_loss, head_grad)


def solution(mesh):
    in_specs = (
        P(AXES, None),
        P(AXES, None),
        P(),
        P(),
        P(AXES, None),
        P(AXES),
        P(AXES),
    )
    out_specs = (P(AXES, None), P(AXES), P(AXES, None))
    return jax.shard_map(shards, mesh=mesh, in_specs=in_specs, out_specs=out_specs, check_vma=False)
```

```python
import jax
import jax.numpy as jnp
from jax import lax
from jax.experimental import pallas as pl
from jax.sharding import PartitionSpec as P

D = 2048
BLOCK = 128
SB = 8
LB = 6
CAP = 4
EXTRA = 128
LABEL_SPLIT = 128

SMOOTH = 0.1
AXES = ("vocab", "fsdp")
GROUPS_PER_STEP = 128


def _place(lang_ref, owner_ref, labels_ref, weights_ref, hidden_ref, o_ref, target_ref):
    tokens = hidden_ref.shape[0]
    languages = owner_ref.shape[0]
    lang = lang_ref[...].reshape(1, tokens)
    owner = owner_ref[...].reshape(1, languages)
    is_lang = (lax.broadcasted_iota(jnp.int32, (languages, tokens), 0) == lang).astype(
        jnp.bfloat16
    )
    same = lax.dot_general(
        is_lang, is_lang, (((0,), (0,)), ((), ())), preferred_element_type=jnp.float32
    )
    before = lax.broadcasted_iota(jnp.int32, (tokens, tokens), 0) < lax.broadcasted_iota(
        jnp.int32, (tokens, tokens), 1
    )
    rank = jnp.sum(jnp.where(before, same, 0.0), axis=0, keepdims=True)
    slot = jnp.dot(owner.astype(jnp.bfloat16), is_lang, preferred_element_type=jnp.float32)
    target = (slot * CAP + rank).astype(jnp.int32)
    target_ref[...] = target
    labels = labels_ref[...].reshape(1, tokens)
    kind = lax.broadcasted_iota(jnp.int32, (EXTRA, tokens), 0)
    extras_t = jnp.where(
        kind == 0,
        weights_ref[...].reshape(1, tokens).astype(jnp.float32),
        jnp.where(
            kind == 1,
            (labels // LABEL_SPLIT).astype(jnp.float32),
            jnp.where(kind == 2, (labels % LABEL_SPLIT).astype(jnp.float32), 0.0),
        ),
    ).astype(jnp.bfloat16)
    step_rows = o_ref.shape[0] * o_ref.shape[1]
    first = pl.program_id(0) * step_rows
    hot = (lax.broadcasted_iota(jnp.int32, (step_rows, tokens), 0) + first == target).astype(
        jnp.bfloat16
    )
    rows = jnp.dot(hot, hidden_ref[...], preferred_element_type=jnp.float32)
    extra = lax.dot_general(
        hot, extras_t, (((1,), (1,)), ((), ())), preferred_element_type=jnp.float32
    )
    out = jnp.concatenate([rows.astype(jnp.bfloat16), extra.astype(jnp.bfloat16)], axis=1)
    o_ref[...] = out.reshape(o_ref.shape)


def place(token_language, language_owner, labels, loss_weight, hidden, groups):
    tokens, features = hidden.shape
    languages = language_owner.shape[0]
    width = features + EXTRA
    step = min(GROUPS_PER_STEP, groups)
    whole = lambda i: (0,)
    return pl.pallas_call(
        _place,
        grid=(groups // step,),
        in_specs=[
            pl.BlockSpec((tokens,), whole),
            pl.BlockSpec((languages,), whole),
            pl.BlockSpec((tokens,), whole),
            pl.BlockSpec((tokens,), whole),
            pl.BlockSpec((tokens, features), lambda i: (0, 0)),
        ],
        out_specs=[
            pl.BlockSpec((step, CAP, width), lambda i: (i, 0, 0)),
            pl.BlockSpec((1, tokens), lambda i: (0, 0)),
        ],
        out_shape=[
            jax.ShapeDtypeStruct((groups, CAP, width), hidden.dtype),
            jax.ShapeDtypeStruct((1, tokens), jnp.int32),
        ],
    )(token_language.reshape(tokens), language_owner, labels, loss_weight, hidden)


def _unplace(target_ref, r_ref, rows_ref, loss_ref):
    x = r_ref[...]
    x = x.reshape(x.shape[0] * x.shape[1], x.shape[2])
    tokens = target_ref.shape[1]
    features = rows_ref.shape[1]
    hot_t = (lax.broadcasted_iota(jnp.int32, (x.shape[0], tokens), 0) == target_ref[...]).astype(
        jnp.bfloat16
    )
    rows = lax.dot_general(
        hot_t, x[:, :features], (((0,), (0,)), ((), ())), preferred_element_type=jnp.float32
    )
    rows_ref[...] = rows.astype(rows_ref.dtype)
    loss = lax.dot_general(
        x[:, features:], hot_t, (((0,), (0,)), ((), ())), preferred_element_type=jnp.float32
    )
    loss_ref[...] = loss[0:1, :].astype(loss_ref.dtype).reshape(loss_ref.shape)


def unplace(target_row, returned, features):
    groups, cap, width = returned.shape
    tokens = target_row.shape[1]
    return pl.pallas_call(
        _unplace,
        grid=(1,),
        in_specs=[
            pl.BlockSpec((1, tokens), lambda i: (0, 0)),
            pl.BlockSpec((groups, cap, width), lambda i: (0, 0, 0)),
        ],
        out_specs=[
            pl.BlockSpec((tokens, features), lambda i: (0, 0)),
            pl.BlockSpec((tokens,), lambda i: (0,)),
        ],
        out_shape=[
            jax.ShapeDtypeStruct((tokens, features), returned.dtype),
            jax.ShapeDtypeStruct((tokens,), returned.dtype),
        ],
    )(target_row, returned)


def _middle(r_ref, cand_ref, back_ref, grads_ref):
    x = r_ref[...]
    x = x.reshape(x.shape[0] * x.shape[1], x.shape[2])
    n, width = x.shape
    cand = cand_ref[...]
    columns, features = cand.shape
    logits = lax.dot_general(
        x[:, :features], cand, (((1,), (1,)), ((), ())), preferred_element_type=jnp.float32
    )
    weights = x[:, features : features + 1].astype(jnp.float32)
    targets = (
        x[:, features + 1 : features + 2].astype(jnp.float32) * LABEL_SPLIT
        + x[:, features + 2 : features + 3].astype(jnp.float32)
    ).astype(jnp.int32)
    row_max = jnp.max(logits, axis=1, keepdims=True)
    shifted = logits - row_max
    exps = jnp.exp(shifted)
    total = jnp.sum(exps, axis=1, keepdims=True)
    log_probs = shifted - jnp.log(total)
    onehot = (lax.broadcasted_iota(jnp.int32, logits.shape, 1) == targets).astype(jnp.float32)
    losses = -(1.0 - SMOOTH) * jnp.sum(onehot * log_probs, axis=1, keepdims=True) - (
        SMOOTH / columns
    ) * jnp.sum(log_probs, axis=1, keepdims=True)
    probs = exps * (1.0 / total)
    grads = (weights * (probs - (1.0 - SMOOTH) * onehot - SMOOTH / columns)).astype(jnp.bfloat16)
    grads_ref[...] = grads
    row_grads = jnp.dot(grads, cand, preferred_element_type=jnp.float32).astype(jnp.bfloat16)
    extras = jnp.where(
        lax.broadcasted_iota(jnp.int32, (n, width - features), 1) == 0,
        losses.astype(jnp.bfloat16),
        jnp.zeros((), jnp.bfloat16),
    )
    back = jnp.concatenate([row_grads, extras], axis=1)
    back_ref[...] = back.reshape(back_ref.shape)


def middle(received, candidates):
    groups, cap, width = received.shape
    columns, features = candidates.shape
    step = min(GROUPS_PER_STEP, groups)
    return pl.pallas_call(
        _middle,
        grid=(groups // step,),
        in_specs=[
            pl.BlockSpec((step, cap, width), lambda i: (i, 0, 0)),
            pl.BlockSpec((columns, features), lambda i: (0, 0)),
        ],
        out_specs=[
            pl.BlockSpec((step, cap, width), lambda i: (i, 0, 0)),
            pl.BlockSpec((step * cap, columns), lambda i: (i, 0)),
        ],
        out_shape=[
            jax.ShapeDtypeStruct((groups, cap, width), received.dtype),
            jax.ShapeDtypeStruct((groups * cap, columns), jnp.bfloat16),
        ],
    )(received, candidates)


def shards(
    hidden, head_weight, language_blocks, language_owner, token_language, labels, loss_weight
):
    devices = lax.axis_size(AXES)
    tokens, features = hidden.shape
    places = devices * CAP
    assert head_weight.shape[0] == SB * BLOCK

    send, target_row = place(token_language, language_owner, labels, loss_weight, hidden, devices)
    received = lax.all_to_all(send, AXES, split_axis=0, concat_axis=0, tiled=True)

    self_index = lax.axis_index(AXES)
    owned_mask = (language_owner == self_index).astype(jnp.int32)
    blocks = jnp.sum(owned_mask[:, None] * language_blocks, axis=0)
    slab = head_weight.reshape(SB, BLOCK, features)
    candidates = jnp.take(slab, blocks, axis=0).reshape(LB * BLOCK, features)

    back, grads = middle(received, candidates)
    returned = lax.all_to_all(back, AXES, split_axis=0, concat_axis=0, tiled=True)
    received, grads = lax.optimization_barrier((received, grads))
    token_rows = received.reshape(places, received.shape[2])

    block_hot = blocks[None, :] == jnp.arange(SB, dtype=jnp.int32)[:, None]
    listed = jnp.any(block_hot, axis=1)
    list_index = jnp.sum(
        jnp.where(block_hot, jnp.arange(LB, dtype=jnp.int32)[None, :], 0), axis=1
    )
    grads_by_block = grads.reshape(places, LB, BLOCK)
    expanded = jnp.where(
        listed[None, :, None],
        jnp.take(grads_by_block, list_index, axis=1),
        jnp.zeros((), jnp.bfloat16),
    ).reshape(places, SB * BLOCK)
    head_grad = lax.dot_general(
        expanded, token_rows[:, :features], (((0,), (0,)), ((), ())),
        preferred_element_type=jnp.float32,
    ).astype(jnp.bfloat16)

    hidden_grad, token_loss = unplace(target_row, returned, features)
    return (hidden_grad, token_loss, head_grad)


def solution(mesh):
    in_specs = (
        P(AXES, None),
        P(AXES, None),
        P(),
        P(),
        P(AXES, None),
        P(AXES),
        P(AXES),
    )
    out_specs = (P(AXES, None), P(AXES), P(AXES, None))
    return jax.shard_map(shards, mesh=mesh, in_specs=in_specs, out_specs=out_specs, check_vma=False)
```

```python
import jax
import jax.numpy as jnp
from jax import lax
from jax.experimental import pallas as pl
from jax.experimental.pallas import tpu as pltpu
from jax.sharding import PartitionSpec as P

D = 2048
BLOCK = 128
SB = 8
LB = 6
CAP = 4
EXTRA = 128
LABEL_SPLIT = 128

SMOOTH = 0.1
AXES = ("vocab", "fsdp")
GROUPS_PER_STEP = 128


def _place(lang_ref, owner_ref, labels_ref, weights_ref, hidden_ref, o_ref, target_ref, extras_ref):
    tokens = hidden_ref.shape[0]
    languages = owner_ref.shape[0]

    @pl.when(pl.program_id(0) == 0)
    def _():
        lang = lang_ref[...].reshape(1, tokens)
        owner = owner_ref[...].reshape(1, languages)
        is_lang = (lax.broadcasted_iota(jnp.int32, (languages, tokens), 0) == lang).astype(
            jnp.bfloat16
        )
        same = lax.dot_general(
            is_lang, is_lang, (((0,), (0,)), ((), ())), preferred_element_type=jnp.float32
        )
        before = lax.broadcasted_iota(jnp.int32, (tokens, tokens), 0) < lax.broadcasted_iota(
            jnp.int32, (tokens, tokens), 1
        )
        rank = jnp.sum(jnp.where(before, same, 0.0), axis=0, keepdims=True)
        slot = jnp.dot(owner.astype(jnp.bfloat16), is_lang, preferred_element_type=jnp.float32)
        target_ref[...] = (slot * CAP + rank).astype(jnp.int32)
        labels = labels_ref[...].reshape(1, tokens)
        kind = lax.broadcasted_iota(jnp.int32, (EXTRA, tokens), 0)
        extras_ref[...] = jnp.where(
            kind == 0,
            weights_ref[...].reshape(1, tokens).astype(jnp.float32),
            jnp.where(
                kind == 1,
                (labels // LABEL_SPLIT).astype(jnp.float32),
                jnp.where(kind == 2, (labels % LABEL_SPLIT).astype(jnp.float32), 0.0),
            ),
        ).astype(jnp.bfloat16)

    step_rows = o_ref.shape[0] * o_ref.shape[1]
    first = pl.program_id(0) * step_rows
    hot = (
        lax.broadcasted_iota(jnp.int32, (step_rows, tokens), 0) + first == target_ref[...]
    ).astype(jnp.bfloat16)
    rows = jnp.dot(hot, hidden_ref[...], preferred_element_type=jnp.float32)
    extra = lax.dot_general(
        hot, extras_ref[...], (((1,), (1,)), ((), ())), preferred_element_type=jnp.float32
    )
    out = jnp.concatenate([rows.astype(jnp.bfloat16), extra.astype(jnp.bfloat16)], axis=1)
    o_ref[...] = out.reshape(o_ref.shape)


def place(token_language, language_owner, labels, loss_weight, hidden, groups):
    tokens, features = hidden.shape
    languages = language_owner.shape[0]
    width = features + EXTRA
    step = min(GROUPS_PER_STEP, groups)
    whole = lambda i: (0,)
    return pl.pallas_call(
        _place,
        grid=(groups // step,),
        in_specs=[
            pl.BlockSpec((tokens,), whole),
            pl.BlockSpec((languages,), whole),
            pl.BlockSpec((tokens,), whole),
            pl.BlockSpec((tokens,), whole),
            pl.BlockSpec((tokens, features), lambda i: (0, 0)),
        ],
        out_specs=[
            pl.BlockSpec((step, CAP, width), lambda i: (i, 0, 0)),
            pl.BlockSpec((1, tokens), lambda i: (0, 0)),
        ],
        out_shape=[
            jax.ShapeDtypeStruct((groups, CAP, width), hidden.dtype),
            jax.ShapeDtypeStruct((1, tokens), jnp.int32),
        ],
        scratch_shapes=[pltpu.VMEM((EXTRA, tokens), jnp.bfloat16)],
    )(token_language.reshape(tokens), language_owner, labels, loss_weight, hidden)


def _unplace(target_ref, r_ref, rows_ref, loss_ref):
    x = r_ref[...]
    x = x.reshape(x.shape[0] * x.shape[1], x.shape[2])
    tokens = target_ref.shape[1]
    features = rows_ref.shape[1]
    hot_t = (lax.broadcasted_iota(jnp.int32, (x.shape[0], tokens), 0) == target_ref[...]).astype(
        jnp.bfloat16
    )
    rows = lax.dot_general(
        hot_t, x[:, :features], (((0,), (0,)), ((), ())), preferred_element_type=jnp.float32
    )
    rows_ref[...] = rows.astype(rows_ref.dtype)
    loss = lax.dot_general(
        x[:, features:], hot_t, (((0,), (0,)), ((), ())), preferred_element_type=jnp.float32
    )
    loss_ref[...] = loss[0:1, :].astype(loss_ref.dtype).reshape(loss_ref.shape)


def unplace(target_row, returned, features):
    groups, cap, width = returned.shape
    tokens = target_row.shape[1]
    return pl.pallas_call(
        _unplace,
        grid=(1,),
        in_specs=[
            pl.BlockSpec((1, tokens), lambda i: (0, 0)),
            pl.BlockSpec((groups, cap, width), lambda i: (0, 0, 0)),
        ],
        out_specs=[
            pl.BlockSpec((tokens, features), lambda i: (0, 0)),
            pl.BlockSpec((tokens,), lambda i: (0,)),
        ],
        out_shape=[
            jax.ShapeDtypeStruct((tokens, features), returned.dtype),
            jax.ShapeDtypeStruct((tokens,), returned.dtype),
        ],
    )(target_row, returned)


def _middle(r_ref, cand_ref, back_ref, rows_ref, grads_ref):
    x = r_ref[...]
    x = x.reshape(x.shape[0] * x.shape[1], x.shape[2])
    rows_ref[...] = x
    n, width = x.shape
    cand = cand_ref[...]
    columns, features = cand.shape
    logits = lax.dot_general(
        x[:, :features], cand, (((1,), (1,)), ((), ())), preferred_element_type=jnp.float32
    )
    weights = x[:, features : features + 1].astype(jnp.float32)
    targets = (
        x[:, features + 1 : features + 2].astype(jnp.float32) * LABEL_SPLIT
        + x[:, features + 2 : features + 3].astype(jnp.float32)
    ).astype(jnp.int32)
    row_max = jnp.max(logits, axis=1, keepdims=True)
    shifted = logits - row_max
    exps = jnp.exp(shifted)
    total = jnp.sum(exps, axis=1, keepdims=True)
    log_probs = shifted - jnp.log(total)
    onehot = (lax.broadcasted_iota(jnp.int32, logits.shape, 1) == targets).astype(jnp.float32)
    losses = -(1.0 - SMOOTH) * jnp.sum(onehot * log_probs, axis=1, keepdims=True) - (
        SMOOTH / columns
    ) * jnp.sum(log_probs, axis=1, keepdims=True)
    probs = exps * (1.0 / total)
    grads = (weights * (probs - (1.0 - SMOOTH) * onehot - SMOOTH / columns)).astype(jnp.bfloat16)
    grads_ref[...] = grads
    row_grads = jnp.dot(grads, cand, preferred_element_type=jnp.float32).astype(jnp.bfloat16)
    extras = jnp.where(
        lax.broadcasted_iota(jnp.int32, (n, width - features), 1) == 0,
        losses.astype(jnp.bfloat16),
        jnp.zeros((), jnp.bfloat16),
    )
    back = jnp.concatenate([row_grads, extras], axis=1)
    back_ref[...] = back.reshape(back_ref.shape)


def middle(received, candidates):
    groups, cap, width = received.shape
    columns, features = candidates.shape
    step = min(GROUPS_PER_STEP, groups)
    return pl.pallas_call(
        _middle,
        grid=(groups // step,),
        in_specs=[
            pl.BlockSpec((step, cap, width), lambda i: (i, 0, 0)),
            pl.BlockSpec((columns, features), lambda i: (0, 0)),
        ],
        out_specs=[
            pl.BlockSpec((step, cap, width), lambda i: (i, 0, 0)),
            pl.BlockSpec((step * cap, width), lambda i: (i, 0)),
            pl.BlockSpec((step * cap, columns), lambda i: (i, 0)),
        ],
        out_shape=[
            jax.ShapeDtypeStruct((groups, cap, width), received.dtype),
            jax.ShapeDtypeStruct((groups * cap, width), received.dtype),
            jax.ShapeDtypeStruct((groups * cap, columns), jnp.bfloat16),
        ],
    )(received, candidates)


def shards(
    hidden, head_weight, language_blocks, language_owner, token_language, labels, loss_weight
):
    devices = lax.axis_size(AXES)
    tokens, features = hidden.shape
    places = devices * CAP
    assert head_weight.shape[0] == SB * BLOCK

    send, target_row = place(token_language, language_owner, labels, loss_weight, hidden, devices)
    received = lax.all_to_all(send, AXES, split_axis=0, concat_axis=0, tiled=True)

    self_index = lax.axis_index(AXES)
    owned_mask = (language_owner == self_index).astype(jnp.int32)
    blocks = jnp.sum(owned_mask[:, None] * language_blocks, axis=0)
    slab = head_weight.reshape(SB, BLOCK, features)
    candidates = jnp.take(slab, blocks, axis=0).reshape(LB * BLOCK, features)

    back, token_rows, grads = middle(received, candidates)
    returned = lax.all_to_all(back, AXES, split_axis=0, concat_axis=0, tiled=True)

    block_hot = blocks[None, :] == jnp.arange(SB, dtype=jnp.int32)[:, None]
    listed = jnp.any(block_hot, axis=1)
    list_index = jnp.sum(
        jnp.where(block_hot, jnp.arange(LB, dtype=jnp.int32)[None, :], 0), axis=1
    )
    grads_by_block = grads.reshape(places, LB, BLOCK)
    expanded = jnp.where(
        listed[None, :, None],
        jnp.take(grads_by_block, list_index, axis=1),
        jnp.zeros((), jnp.bfloat16),
    ).reshape(places, SB * BLOCK)
    head_grad = lax.dot_general(
        expanded, token_rows[:, :features], (((0,), (0,)), ((), ())),
        preferred_element_type=jnp.float32,
    ).astype(jnp.bfloat16)

    hidden_grad, token_loss = unplace(target_row, returned, features)
    return (hidden_grad, token_loss, head_grad)


def solution(mesh):
    in_specs = (
        P(AXES, None),
        P(AXES, None),
        P(),
        P(),
        P(AXES, None),
        P(AXES),
        P(AXES),
    )
    out_specs = (P(AXES, None), P(AXES), P(AXES, None))
    return jax.shard_map(shards, mesh=mesh, in_specs=in_specs, out_specs=out_specs, check_vma=False)
```

```python
import jax
import jax.numpy as jnp
from jax import lax
from jax.experimental import pallas as pl
from jax.experimental.pallas import tpu as pltpu
from jax.sharding import PartitionSpec as P

D = 2048
BLOCK = 128
SB = 8
LB = 6
CAP = 4
EXTRA = 128
LABEL_SPLIT = 128

SMOOTH = 0.1
AXES = ("vocab", "fsdp")
GROUPS_PER_STEP = 128


def _place(
    lang_ref, owner_ref, labels_ref, weights_ref, hidden_ref, o_ref, target_ref, column_ref,
    extras_ref,
):
    tokens = hidden_ref.shape[0]
    languages = owner_ref.shape[0]

    @pl.when(pl.program_id(0) == 0)
    def _():
        lang = lang_ref[...].reshape(1, tokens)
        owner = owner_ref[...].reshape(1, languages)
        is_lang = (lax.broadcasted_iota(jnp.int32, (languages, tokens), 0) == lang).astype(
            jnp.bfloat16
        )
        same = lax.dot_general(
            is_lang, is_lang, (((0,), (0,)), ((), ())), preferred_element_type=jnp.float32
        )
        before = lax.broadcasted_iota(jnp.int32, (tokens, tokens), 0) < lax.broadcasted_iota(
            jnp.int32, (tokens, tokens), 1
        )
        rank = jnp.sum(jnp.where(before, same, 0.0), axis=0, keepdims=True)
        slot = jnp.dot(owner.astype(jnp.bfloat16), is_lang, preferred_element_type=jnp.float32)
        target_ref[...] = (slot * CAP + rank).astype(jnp.int32)
        rank_column = jnp.sum(jnp.where(before, 0.0, same) - jnp.where(
            lax.broadcasted_iota(jnp.int32, (tokens, tokens), 0)
            == lax.broadcasted_iota(jnp.int32, (tokens, tokens), 1), same, 0.0), axis=1, keepdims=True)
        slot_column = lax.dot_general(
            is_lang, owner.astype(jnp.bfloat16), (((0,), (1,)), ((), ())),
            preferred_element_type=jnp.float32,
        )
        column_ref[...] = (slot_column * CAP + rank_column).astype(jnp.int32)
        labels = labels_ref[...].reshape(1, tokens)
        kind = lax.broadcasted_iota(jnp.int32, (EXTRA, tokens), 0)
        extras_ref[...] = jnp.where(
            kind == 0,
            weights_ref[...].reshape(1, tokens).astype(jnp.float32),
            jnp.where(
                kind == 1,
                (labels // LABEL_SPLIT).astype(jnp.float32),
                jnp.where(kind == 2, (labels % LABEL_SPLIT).astype(jnp.float32), 0.0),
            ),
        ).astype(jnp.bfloat16)

    step_rows = o_ref.shape[0] * o_ref.shape[1]
    first = pl.program_id(0) * step_rows
    hot = (
        lax.broadcasted_iota(jnp.int32, (step_rows, tokens), 0) + first == target_ref[...]
    ).astype(jnp.bfloat16)
    rows = jnp.dot(hot, hidden_ref[...], preferred_element_type=jnp.float32)
    extra = lax.dot_general(
        hot, extras_ref[...], (((1,), (1,)), ((), ())), preferred_element_type=jnp.float32
    )
    out = jnp.concatenate([rows.astype(jnp.bfloat16), extra.astype(jnp.bfloat16)], axis=1)
    o_ref[...] = out.reshape(o_ref.shape)


def place(token_language, language_owner, labels, loss_weight, hidden, groups):
    tokens, features = hidden.shape
    languages = language_owner.shape[0]
    width = features + EXTRA
    step = min(GROUPS_PER_STEP, groups)
    whole = lambda i: (0,)
    return pl.pallas_call(
        _place,
        grid=(groups // step,),
        in_specs=[
            pl.BlockSpec((tokens,), whole),
            pl.BlockSpec((languages,), whole),
            pl.BlockSpec((tokens,), whole),
            pl.BlockSpec((tokens,), whole),
            pl.BlockSpec((tokens, features), lambda i: (0, 0)),
        ],
        out_specs=[
            pl.BlockSpec((step, CAP, width), lambda i: (i, 0, 0)),
            pl.BlockSpec((1, tokens), lambda i: (0, 0)),
            pl.BlockSpec((tokens, 1), lambda i: (0, 0)),
        ],
        out_shape=[
            jax.ShapeDtypeStruct((groups, CAP, width), hidden.dtype),
            jax.ShapeDtypeStruct((1, tokens), jnp.int32),
            jax.ShapeDtypeStruct((tokens, 1), jnp.int32),
        ],
        scratch_shapes=[pltpu.VMEM((EXTRA, tokens), jnp.bfloat16)],
    )(token_language.reshape(tokens), language_owner, labels, loss_weight, hidden)


def _unplace(target_ref, column_ref, r_ref, rows_ref, loss_ref):
    x = r_ref[...]
    x = x.reshape(x.shape[0] * x.shape[1], x.shape[2])
    tokens = target_ref.shape[1]
    features = rows_ref.shape[1]
    hot = (
        lax.broadcasted_iota(jnp.int32, (tokens, x.shape[0]), 1) == column_ref[...]
    ).astype(jnp.bfloat16)
    rows = jnp.dot(hot, x[:, :features], preferred_element_type=jnp.float32)
    rows_ref[...] = rows.astype(rows_ref.dtype)
    hot_t = (lax.broadcasted_iota(jnp.int32, (x.shape[0], tokens), 0) == target_ref[...]).astype(
        jnp.bfloat16
    )
    loss = lax.dot_general(
        x[:, features:], hot_t, (((0,), (0,)), ((), ())), preferred_element_type=jnp.float32
    )
    loss_ref[...] = loss[0:1, :].astype(loss_ref.dtype).reshape(loss_ref.shape)


def unplace(target_row, target_column, returned, features):
    groups, cap, width = returned.shape
    tokens = target_row.shape[1]
    return pl.pallas_call(
        _unplace,
        grid=(1,),
        in_specs=[
            pl.BlockSpec((1, tokens), lambda i: (0, 0)),
            pl.BlockSpec((tokens, 1), lambda i: (0, 0)),
            pl.BlockSpec((groups, cap, width), lambda i: (0, 0, 0)),
        ],
        out_specs=[
            pl.BlockSpec((tokens, features), lambda i: (0, 0)),
            pl.BlockSpec((tokens,), lambda i: (0,)),
        ],
        out_shape=[
            jax.ShapeDtypeStruct((tokens, features), returned.dtype),
            jax.ShapeDtypeStruct((tokens,), returned.dtype),
        ],
    )(target_row, target_column, returned)


def _middle(r_ref, cand_ref, back_ref, rows_ref, grads_ref):
    x = r_ref[...]
    x = x.reshape(x.shape[0] * x.shape[1], x.shape[2])
    rows_ref[...] = x
    n, width = x.shape
    cand = cand_ref[...]
    columns, features = cand.shape
    logits = lax.dot_general(
        x[:, :features], cand, (((1,), (1,)), ((), ())), preferred_element_type=jnp.float32
    )
    weights = x[:, features : features + 1].astype(jnp.float32)
    targets = (
        x[:, features + 1 : features + 2].astype(jnp.float32) * LABEL_SPLIT
        + x[:, features + 2 : features + 3].astype(jnp.float32)
    ).astype(jnp.int32)
    row_max = jnp.max(logits, axis=1, keepdims=True)
    shifted = logits - row_max
    exps = jnp.exp(shifted)
    total = jnp.sum(exps, axis=1, keepdims=True)
    log_probs = shifted - jnp.log(total)
    onehot = (lax.broadcasted_iota(jnp.int32, logits.shape, 1) == targets).astype(jnp.float32)
    losses = -(1.0 - SMOOTH) * jnp.sum(onehot * log_probs, axis=1, keepdims=True) - (
        SMOOTH / columns
    ) * jnp.sum(log_probs, axis=1, keepdims=True)
    probs = exps * (1.0 / total)
    grads = (weights * (probs - (1.0 - SMOOTH) * onehot - SMOOTH / columns)).astype(jnp.bfloat16)
    grads_ref[...] = grads
    row_grads = jnp.dot(grads, cand, preferred_element_type=jnp.float32).astype(jnp.bfloat16)
    extras = jnp.where(
        lax.broadcasted_iota(jnp.int32, (n, width - features), 1) == 0,
        losses.astype(jnp.bfloat16),
        jnp.zeros((), jnp.bfloat16),
    )
    back = jnp.concatenate([row_grads, extras], axis=1)
    back_ref[...] = back.reshape(back_ref.shape)


def middle(received, candidates):
    groups, cap, width = received.shape
    columns, features = candidates.shape
    step = min(GROUPS_PER_STEP, groups)
    return pl.pallas_call(
        _middle,
        grid=(groups // step,),
        in_specs=[
            pl.BlockSpec((step, cap, width), lambda i: (i, 0, 0)),
            pl.BlockSpec((columns, features), lambda i: (0, 0)),
        ],
        out_specs=[
            pl.BlockSpec((step, cap, width), lambda i: (i, 0, 0)),
            pl.BlockSpec((step * cap, width), lambda i: (i, 0)),
            pl.BlockSpec((step * cap, columns), lambda i: (i, 0)),
        ],
        out_shape=[
            jax.ShapeDtypeStruct((groups, cap, width), received.dtype),
            jax.ShapeDtypeStruct((groups * cap, width), received.dtype),
            jax.ShapeDtypeStruct((groups * cap, columns), jnp.bfloat16),
        ],
    )(received, candidates)


def shards(
    hidden, head_weight, language_blocks, language_owner, token_language, labels, loss_weight
):
    devices = lax.axis_size(AXES)
    tokens, features = hidden.shape
    places = devices * CAP
    assert head_weight.shape[0] == SB * BLOCK

    send, target_row, target_column = place(token_language, language_owner, labels, loss_weight, hidden, devices)
    received = lax.all_to_all(send, AXES, split_axis=0, concat_axis=0, tiled=True)

    self_index = lax.axis_index(AXES)
    owned_mask = (language_owner == self_index).astype(jnp.int32)
    blocks = jnp.sum(owned_mask[:, None] * language_blocks, axis=0)
    slab = head_weight.reshape(SB, BLOCK, features)
    candidates = jnp.take(slab, blocks, axis=0).reshape(LB * BLOCK, features)

    back, token_rows, grads = middle(received, candidates)
    returned = lax.all_to_all(back, AXES, split_axis=0, concat_axis=0, tiled=True)

    block_hot = blocks[None, :] == jnp.arange(SB, dtype=jnp.int32)[:, None]
    listed = jnp.any(block_hot, axis=1)
    list_index = jnp.sum(
        jnp.where(block_hot, jnp.arange(LB, dtype=jnp.int32)[None, :], 0), axis=1
    )
    grads_by_block = grads.reshape(places, LB, BLOCK)
    expanded = jnp.where(
        listed[None, :, None],
        jnp.take(grads_by_block, list_index, axis=1),
        jnp.zeros((), jnp.bfloat16),
    ).reshape(places, SB * BLOCK)
    head_grad = lax.dot_general(
        expanded, token_rows[:, :features], (((0,), (0,)), ((), ())),
        preferred_element_type=jnp.float32,
    ).astype(jnp.bfloat16)

    hidden_grad, token_loss = unplace(target_row, target_column, returned, features)
    return (hidden_grad, token_loss, head_grad)


def solution(mesh):
    in_specs = (
        P(AXES, None),
        P(AXES, None),
        P(),
        P(),
        P(AXES, None),
        P(AXES),
        P(AXES),
    )
    out_specs = (P(AXES, None), P(AXES), P(AXES, None))
    return jax.shard_map(shards, mesh=mesh, in_specs=in_specs, out_specs=out_specs, check_vma=False)
```

```python
import jax
import jax.numpy as jnp
from jax import lax
from jax.experimental import pallas as pl
from jax.experimental.pallas import tpu as pltpu
from jax.sharding import PartitionSpec as P

D = 2048
BLOCK = 128
SB = 8
LB = 6
CAP = 4
EXTRA = 128
LABEL_SPLIT = 128

SMOOTH = 0.1
AXES = ("vocab", "fsdp")
GROUPS_PER_STEP = 128


def _place(lang_ref, owner_ref, labels_ref, weights_ref, hidden_ref, o_ref, target_ref, extras_ref):
    tokens = hidden_ref.shape[0]
    languages = owner_ref.shape[0]

    @pl.when(pl.program_id(0) == 0)
    def _():
        lang = lang_ref[...].reshape(1, tokens)
        owner = owner_ref[...].reshape(1, languages)
        is_lang = (lax.broadcasted_iota(jnp.int32, (languages, tokens), 0) == lang).astype(
            jnp.bfloat16
        )
        same = lax.dot_general(
            is_lang, is_lang, (((0,), (0,)), ((), ())), preferred_element_type=jnp.float32
        )
        before = lax.broadcasted_iota(jnp.int32, (tokens, tokens), 0) < lax.broadcasted_iota(
            jnp.int32, (tokens, tokens), 1
        )
        rank = jnp.sum(jnp.where(before, same, 0.0), axis=0, keepdims=True)
        slot = jnp.dot(owner.astype(jnp.bfloat16), is_lang, preferred_element_type=jnp.float32)
        target_ref[...] = (slot * CAP + rank).astype(jnp.int32)
        labels = labels_ref[...].reshape(1, tokens)
        kind = lax.broadcasted_iota(jnp.int32, (EXTRA, tokens), 0)
        extras_ref[...] = jnp.where(
            kind == 0,
            weights_ref[...].reshape(1, tokens).astype(jnp.float32),
            jnp.where(
                kind == 1,
                (labels // LABEL_SPLIT).astype(jnp.float32),
                jnp.where(kind == 2, (labels % LABEL_SPLIT).astype(jnp.float32), 0.0),
            ),
        ).astype(jnp.bfloat16)

    step_rows = o_ref.shape[0] * o_ref.shape[1]
    first = pl.program_id(0) * step_rows
    hot = (
        lax.broadcasted_iota(jnp.int32, (step_rows, tokens), 0) + first == target_ref[...]
    ).astype(jnp.bfloat16)
    rows = jnp.dot(hot, hidden_ref[...], preferred_element_type=jnp.float32)
    extra = lax.dot_general(
        hot, extras_ref[...], (((1,), (1,)), ((), ())), preferred_element_type=jnp.float32
    )
    out = jnp.concatenate([rows.astype(jnp.bfloat16), extra.astype(jnp.bfloat16)], axis=1)
    o_ref[...] = out.reshape(o_ref.shape)


def place(token_language, language_owner, labels, loss_weight, hidden, groups):
    tokens, features = hidden.shape
    languages = language_owner.shape[0]
    width = features + EXTRA
    step = min(GROUPS_PER_STEP, groups)
    whole = lambda i: (0,)
    return pl.pallas_call(
        _place,
        grid=(groups // step,),
        in_specs=[
            pl.BlockSpec((tokens,), whole),
            pl.BlockSpec((languages,), whole),
            pl.BlockSpec((tokens,), whole),
            pl.BlockSpec((tokens,), whole),
            pl.BlockSpec((tokens, features), lambda i: (0, 0)),
        ],
        out_specs=[
            pl.BlockSpec((step, CAP, width), lambda i: (i, 0, 0)),
            pl.BlockSpec((1, tokens), lambda i: (0, 0)),
        ],
        out_shape=[
            jax.ShapeDtypeStruct((groups, CAP, width), hidden.dtype),
            jax.ShapeDtypeStruct((1, tokens), jnp.int32),
        ],
        scratch_shapes=[pltpu.VMEM((EXTRA, tokens), jnp.bfloat16)],
    )(token_language.reshape(tokens), language_owner, labels, loss_weight, hidden)


def _unplace(target_ref, r_ref, rows_ref, loss_ref):
    i = pl.program_id(0)
    x = r_ref[...]
    x = x.reshape(x.shape[0] * x.shape[1], x.shape[2])
    tokens = target_ref.shape[1]
    features = rows_ref.shape[1]
    hot_t = (
        lax.broadcasted_iota(jnp.int32, (x.shape[0], tokens), 0) + i * x.shape[0]
        == target_ref[...]
    ).astype(jnp.bfloat16)
    rows = lax.dot_general(
        hot_t, x[:, :features], (((0,), (0,)), ((), ())), preferred_element_type=jnp.float32
    ).astype(rows_ref.dtype)
    loss = lax.dot_general(
        x[:, features:], hot_t, (((0,), (0,)), ((), ())), preferred_element_type=jnp.float32
    )
    loss = loss[0:1, :].astype(loss_ref.dtype).reshape(loss_ref.shape)

    @pl.when(i == 0)
    def _():
        rows_ref[...] = rows
        loss_ref[...] = loss

    @pl.when(i > 0)
    def _():
        rows_ref[...] = rows_ref[...] + rows
        loss_ref[...] = loss_ref[...] + loss


def unplace(target_row, returned, features):
    groups, cap, width = returned.shape
    tokens = target_row.shape[1]
    step = groups // 2
    return pl.pallas_call(
        _unplace,
        grid=(groups // step,),
        in_specs=[
            pl.BlockSpec((1, tokens), lambda i: (0, 0)),
            pl.BlockSpec((step, cap, width), lambda i: (i, 0, 0)),
        ],
        out_specs=[
            pl.BlockSpec((tokens, features), lambda i: (0, 0)),
            pl.BlockSpec((tokens,), lambda i: (0,)),
        ],
        out_shape=[
            jax.ShapeDtypeStruct((tokens, features), returned.dtype),
            jax.ShapeDtypeStruct((tokens,), returned.dtype),
        ],
    )(target_row, returned)


def _middle(r_ref, cand_ref, back_ref, rows_ref, grads_ref):
    x = r_ref[...]
    x = x.reshape(x.shape[0] * x.shape[1], x.shape[2])
    rows_ref[...] = x
    n, width = x.shape
    cand = cand_ref[...]
    columns, features = cand.shape
    logits = lax.dot_general(
        x[:, :features], cand, (((1,), (1,)), ((), ())), preferred_element_type=jnp.float32
    )
    weights = x[:, features : features + 1].astype(jnp.float32)
    targets = (
        x[:, features + 1 : features + 2].astype(jnp.float32) * LABEL_SPLIT
        + x[:, features + 2 : features + 3].astype(jnp.float32)
    ).astype(jnp.int32)
    row_max = jnp.max(logits, axis=1, keepdims=True)
    shifted = logits - row_max
    exps = jnp.exp(shifted)
    total = jnp.sum(exps, axis=1, keepdims=True)
    log_probs = shifted - jnp.log(total)
    onehot = (lax.broadcasted_iota(jnp.int32, logits.shape, 1) == targets).astype(jnp.float32)
    losses = -(1.0 - SMOOTH) * jnp.sum(onehot * log_probs, axis=1, keepdims=True) - (
        SMOOTH / columns
    ) * jnp.sum(log_probs, axis=1, keepdims=True)
    probs = exps * (1.0 / total)
    grads = (weights * (probs - (1.0 - SMOOTH) * onehot - SMOOTH / columns)).astype(jnp.bfloat16)
    grads_ref[...] = grads
    row_grads = jnp.dot(grads, cand, preferred_element_type=jnp.float32).astype(jnp.bfloat16)
    extras = jnp.where(
        lax.broadcasted_iota(jnp.int32, (n, width - features), 1) == 0,
        losses.astype(jnp.bfloat16),
        jnp.zeros((), jnp.bfloat16),
    )
    back = jnp.concatenate([row_grads, extras], axis=1)
    back_ref[...] = back.reshape(back_ref.shape)


def middle(received, candidates):
    groups, cap, width = received.shape
    columns, features = candidates.shape
    step = min(GROUPS_PER_STEP, groups)
    return pl.pallas_call(
        _middle,
        grid=(groups // step,),
        in_specs=[
            pl.BlockSpec((step, cap, width), lambda i: (i, 0, 0)),
            pl.BlockSpec((columns, features), lambda i: (0, 0)),
        ],
        out_specs=[
            pl.BlockSpec((step, cap, width), lambda i: (i, 0, 0)),
            pl.BlockSpec((step * cap, width), lambda i: (i, 0)),
            pl.BlockSpec((step * cap, columns), lambda i: (i, 0)),
        ],
        out_shape=[
            jax.ShapeDtypeStruct((groups, cap, width), received.dtype),
            jax.ShapeDtypeStruct((groups * cap, width), received.dtype),
            jax.ShapeDtypeStruct((groups * cap, columns), jnp.bfloat16),
        ],
    )(received, candidates)


def shards(
    hidden, head_weight, language_blocks, language_owner, token_language, labels, loss_weight
):
    devices = lax.axis_size(AXES)
    tokens, features = hidden.shape
    places = devices * CAP
    assert head_weight.shape[0] == SB * BLOCK

    send, target_row = place(token_language, language_owner, labels, loss_weight, hidden, devices)
    received = lax.all_to_all(send, AXES, split_axis=0, concat_axis=0, tiled=True)

    self_index = lax.axis_index(AXES)
    owned_mask = (language_owner == self_index).astype(jnp.int32)
    blocks = jnp.sum(owned_mask[:, None] * language_blocks, axis=0)
    slab = head_weight.reshape(SB, BLOCK, features)
    candidates = jnp.take(slab, blocks, axis=0).reshape(LB * BLOCK, features)

    back, token_rows, grads = middle(received, candidates)
    returned = lax.all_to_all(back, AXES, split_axis=0, concat_axis=0, tiled=True)

    block_hot = blocks[None, :] == jnp.arange(SB, dtype=jnp.int32)[:, None]
    listed = jnp.any(block_hot, axis=1)
    list_index = jnp.sum(
        jnp.where(block_hot, jnp.arange(LB, dtype=jnp.int32)[None, :], 0), axis=1
    )
    grads_by_block = grads.reshape(places, LB, BLOCK)
    expanded = jnp.where(
        listed[None, :, None],
        jnp.take(grads_by_block, list_index, axis=1),
        jnp.zeros((), jnp.bfloat16),
    ).reshape(places, SB * BLOCK)
    head_grad = lax.dot_general(
        expanded, token_rows[:, :features], (((0,), (0,)), ((), ())),
        preferred_element_type=jnp.float32,
    ).astype(jnp.bfloat16)

    hidden_grad, token_loss = unplace(target_row, returned, features)
    return (hidden_grad, token_loss, head_grad)


def solution(mesh):
    in_specs = (
        P(AXES, None),
        P(AXES, None),
        P(),
        P(),
        P(AXES, None),
        P(AXES),
        P(AXES),
    )
    out_specs = (P(AXES, None), P(AXES), P(AXES, None))
    return jax.shard_map(shards, mesh=mesh, in_specs=in_specs, out_specs=out_specs, check_vma=False)
```

```python
import jax
import jax.numpy as jnp
from jax import lax
from jax.experimental import pallas as pl
from jax.experimental.pallas import tpu as pltpu
from jax.sharding import PartitionSpec as P

D = 2048
BLOCK = 128
SB = 8
LB = 6
CAP = 4
EXTRA = 128
LABEL_SPLIT = 128

SMOOTH = 0.1
AXES = ("vocab", "fsdp")
GROUPS_PER_STEP = 128


def _place(lang_ref, owner_ref, labels_ref, weights_ref, hidden_ref, o_ref, target_ref, extras_ref):
    tokens = hidden_ref.shape[0]
    languages = owner_ref.shape[0]

    @pl.when(pl.program_id(0) == 0)
    def _():
        lang = lang_ref[...].reshape(1, tokens)
        owner = owner_ref[...].reshape(1, languages)
        is_lang = (lax.broadcasted_iota(jnp.int32, (languages, tokens), 0) == lang).astype(
            jnp.bfloat16
        )
        same = lax.dot_general(
            is_lang, is_lang, (((0,), (0,)), ((), ())), preferred_element_type=jnp.float32
        )
        before = lax.broadcasted_iota(jnp.int32, (tokens, tokens), 0) < lax.broadcasted_iota(
            jnp.int32, (tokens, tokens), 1
        )
        rank = jnp.sum(jnp.where(before, same, 0.0), axis=0, keepdims=True)
        slot = jnp.dot(owner.astype(jnp.bfloat16), is_lang, preferred_element_type=jnp.float32)
        target_ref[...] = (slot * CAP + rank).astype(jnp.int32)
        labels = labels_ref[...].reshape(1, tokens)
        kind = lax.broadcasted_iota(jnp.int32, (EXTRA, tokens), 0)
        extras_ref[...] = jnp.where(
            kind == 0,
            weights_ref[...].reshape(1, tokens).astype(jnp.float32),
            jnp.where(
                kind == 1,
                (labels // LABEL_SPLIT).astype(jnp.float32),
                jnp.where(kind == 2, (labels % LABEL_SPLIT).astype(jnp.float32), 0.0),
            ),
        ).astype(jnp.bfloat16)

    step_rows = o_ref.shape[0] * o_ref.shape[1]
    first = pl.program_id(0) * step_rows
    hot = (
        lax.broadcasted_iota(jnp.int32, (step_rows, tokens), 0) + first == target_ref[...]
    ).astype(jnp.bfloat16)
    rows = jnp.dot(hot, hidden_ref[...], preferred_element_type=jnp.float32)
    extra = lax.dot_general(
        hot, extras_ref[...], (((1,), (1,)), ((), ())), preferred_element_type=jnp.float32
    )
    out = jnp.concatenate([rows.astype(jnp.bfloat16), extra.astype(jnp.bfloat16)], axis=1)
    o_ref[...] = out.reshape(o_ref.shape)


def place(token_language, language_owner, labels, loss_weight, hidden, groups):
    tokens, features = hidden.shape
    languages = language_owner.shape[0]
    width = features + EXTRA
    step = groups
    whole = lambda i: (0,)
    return pl.pallas_call(
        _place,
        grid=(groups // step,),
        in_specs=[
            pl.BlockSpec((tokens,), whole),
            pl.BlockSpec((languages,), whole),
            pl.BlockSpec((tokens,), whole),
            pl.BlockSpec((tokens,), whole),
            pl.BlockSpec((tokens, features), lambda i: (0, 0)),
        ],
        out_specs=[
            pl.BlockSpec((step, CAP, width), lambda i: (i, 0, 0)),
            pl.BlockSpec((1, tokens), lambda i: (0, 0)),
        ],
        out_shape=[
            jax.ShapeDtypeStruct((groups, CAP, width), hidden.dtype),
            jax.ShapeDtypeStruct((1, tokens), jnp.int32),
        ],
        scratch_shapes=[pltpu.VMEM((EXTRA, tokens), jnp.bfloat16)],
    )(token_language.reshape(tokens), language_owner, labels, loss_weight, hidden)


def _unplace(target_ref, r_ref, rows_ref, loss_ref):
    x = r_ref[...]
    x = x.reshape(x.shape[0] * x.shape[1], x.shape[2])
    tokens = target_ref.shape[1]
    features = rows_ref.shape[1]
    hot_t = (lax.broadcasted_iota(jnp.int32, (x.shape[0], tokens), 0) == target_ref[...]).astype(
        jnp.bfloat16
    )
    rows = lax.dot_general(
        hot_t, x[:, :features], (((0,), (0,)), ((), ())), preferred_element_type=jnp.float32
    )
    rows_ref[...] = rows.astype(rows_ref.dtype)
    loss = lax.dot_general(
        x[:, features:], hot_t, (((0,), (0,)), ((), ())), preferred_element_type=jnp.float32
    )
    loss_ref[...] = loss[0:1, :].astype(loss_ref.dtype).reshape(loss_ref.shape)


def unplace(target_row, returned, features):
    groups, cap, width = returned.shape
    tokens = target_row.shape[1]
    return pl.pallas_call(
        _unplace,
        grid=(1,),
        in_specs=[
            pl.BlockSpec((1, tokens), lambda i: (0, 0)),
            pl.BlockSpec((groups, cap, width), lambda i: (0, 0, 0)),
        ],
        out_specs=[
            pl.BlockSpec((tokens, features), lambda i: (0, 0)),
            pl.BlockSpec((tokens,), lambda i: (0,)),
        ],
        out_shape=[
            jax.ShapeDtypeStruct((tokens, features), returned.dtype),
            jax.ShapeDtypeStruct((tokens,), returned.dtype),
        ],
    )(target_row, returned)


def _middle(r_ref, cand_ref, back_ref, rows_ref, grads_ref):
    x = r_ref[...]
    x = x.reshape(x.shape[0] * x.shape[1], x.shape[2])
    rows_ref[...] = x
    n, width = x.shape
    cand = cand_ref[...]
    columns, features = cand.shape
    logits = lax.dot_general(
        x[:, :features], cand, (((1,), (1,)), ((), ())), preferred_element_type=jnp.float32
    )
    weights = x[:, features : features + 1].astype(jnp.float32)
    targets = (
        x[:, features + 1 : features + 2].astype(jnp.float32) * LABEL_SPLIT
        + x[:, features + 2 : features + 3].astype(jnp.float32)
    ).astype(jnp.int32)
    row_max = jnp.max(logits, axis=1, keepdims=True)
    shifted = logits - row_max
    exps = jnp.exp(shifted)
    total = jnp.sum(exps, axis=1, keepdims=True)
    log_probs = shifted - jnp.log(total)
    onehot = (lax.broadcasted_iota(jnp.int32, logits.shape, 1) == targets).astype(jnp.float32)
    losses = -(1.0 - SMOOTH) * jnp.sum(onehot * log_probs, axis=1, keepdims=True) - (
        SMOOTH / columns
    ) * jnp.sum(log_probs, axis=1, keepdims=True)
    probs = exps * (1.0 / total)
    grads = (weights * (probs - (1.0 - SMOOTH) * onehot - SMOOTH / columns)).astype(jnp.bfloat16)
    grads_ref[...] = grads
    row_grads = jnp.dot(grads, cand, preferred_element_type=jnp.float32).astype(jnp.bfloat16)
    extras = jnp.where(
        lax.broadcasted_iota(jnp.int32, (n, width - features), 1) == 0,
        losses.astype(jnp.bfloat16),
        jnp.zeros((), jnp.bfloat16),
    )
    back = jnp.concatenate([row_grads, extras], axis=1)
    back_ref[...] = back.reshape(back_ref.shape)


def middle(received, candidates):
    groups, cap, width = received.shape
    columns, features = candidates.shape
    step = min(GROUPS_PER_STEP, groups)
    return pl.pallas_call(
        _middle,
        grid=(groups // step,),
        in_specs=[
            pl.BlockSpec((step, cap, width), lambda i: (i, 0, 0)),
            pl.BlockSpec((columns, features), lambda i: (0, 0)),
        ],
        out_specs=[
            pl.BlockSpec((step, cap, width), lambda i: (i, 0, 0)),
            pl.BlockSpec((step * cap, width), lambda i: (i, 0)),
            pl.BlockSpec((step * cap, columns), lambda i: (i, 0)),
        ],
        out_shape=[
            jax.ShapeDtypeStruct((groups, cap, width), received.dtype),
            jax.ShapeDtypeStruct((groups * cap, width), received.dtype),
            jax.ShapeDtypeStruct((groups * cap, columns), jnp.bfloat16),
        ],
    )(received, candidates)


def shards(
    hidden, head_weight, language_blocks, language_owner, token_language, labels, loss_weight
):
    devices = lax.axis_size(AXES)
    tokens, features = hidden.shape
    places = devices * CAP
    assert head_weight.shape[0] == SB * BLOCK

    send, target_row = place(token_language, language_owner, labels, loss_weight, hidden, devices)
    received = lax.all_to_all(send, AXES, split_axis=0, concat_axis=0, tiled=True)

    self_index = lax.axis_index(AXES)
    owned_mask = (language_owner == self_index).astype(jnp.int32)
    blocks = jnp.sum(owned_mask[:, None] * language_blocks, axis=0)
    slab = head_weight.reshape(SB, BLOCK, features)
    candidates = jnp.take(slab, blocks, axis=0).reshape(LB * BLOCK, features)

    back, token_rows, grads = middle(received, candidates)
    returned = lax.all_to_all(back, AXES, split_axis=0, concat_axis=0, tiled=True)

    block_hot = blocks[None, :] == jnp.arange(SB, dtype=jnp.int32)[:, None]
    listed = jnp.any(block_hot, axis=1)
    list_index = jnp.sum(
        jnp.where(block_hot, jnp.arange(LB, dtype=jnp.int32)[None, :], 0), axis=1
    )
    grads_by_block = grads.reshape(places, LB, BLOCK)
    expanded = jnp.where(
        listed[None, :, None],
        jnp.take(grads_by_block, list_index, axis=1),
        jnp.zeros((), jnp.bfloat16),
    ).reshape(places, SB * BLOCK)
    head_grad = lax.dot_general(
        expanded, token_rows[:, :features], (((0,), (0,)), ((), ())),
        preferred_element_type=jnp.float32,
    ).astype(jnp.bfloat16)

    hidden_grad, token_loss = unplace(target_row, returned, features)
    return (hidden_grad, token_loss, head_grad)


def solution(mesh):
    in_specs = (
        P(AXES, None),
        P(AXES, None),
        P(),
        P(),
        P(AXES, None),
        P(AXES),
        P(AXES),
    )
    out_specs = (P(AXES, None), P(AXES), P(AXES, None))
    return jax.shard_map(shards, mesh=mesh, in_specs=in_specs, out_specs=out_specs, check_vma=False)
```
